256 devices in a mesh: dp: 8 (over x, z_hi), mp: 32 (over z_lo, y, core).
Axes of the slice: x: 4, y: 4, z: 8 (z_hi: 2, z_lo: 4; z = z_hi * 4 + z_lo), core: 2. Of those that a mesh axis runs over, the one named last changes fastest.
Arguments:
- inputs: bfloat16 [4096, 4608], P(('dp', 'mp')), may hold values from -6 to 6
- lengths: int32 [8], P('dp'), may hold values from 1 to 512, as said below
- gain_in: float32 [4608], replicated, may hold values from 0.1 to 1.9
- query_weight: float32 [4608, 4096], P('dp', 'mp'), may hold values from -0.11785113 to 0.11785113
- key_weight: float32 [4608, 2048], P('dp', 'mp'), may hold values from -0.11785113 to 0.11785113
- value_weight: float32 [4608, 2048], P('dp', 'mp'), may hold values from -0.09375 to 0.09375
- output_weight: bfloat16 [4096, 4608], P('mp'), may hold values from -0.09375 to 0.09375
- gain_post: float32 [4608], replicated, may hold values from 0.1 to 1.9
- gain_pre: float32 [4608], replicated, may hold values from 0.1 to 1.9
- gate_weight: float32 [4608, 20480], P('dp', 'mp'), may hold values from -0.09375 to 0.09375
- up_weight: float32 [4608, 20480], P('dp', 'mp'), may hold values from -0.09375 to 0.09375
Outputs:
- residual: bfloat16 [4096, 4608], P(('dp', 'mp'))
- hidden: bfloat16 [4096, 20480], P('dp', 'mp')
- keys_out: bfloat16 [4096, 2048], P('dp', 'mp')
- values_out: bfloat16 [4096, 2048], P('dp', 'mp')
The draws below stay inside these ranges and needn't reach their ends.
Inputs may be any that keep to these rules, and one draw needn't show every extreme that they name: Half of the 8 prompts have lengths under 512 // 16, the others at least 448; at least one prompt fills its slot.
All inputs are finite; a program needn't handle non-finite values.
Results may differ from the reference program's by a relative error of at most 0.03.
Values may be sent and summed in bfloat16 or wider, within the bound.
No kernel may reach another device: no remote copies, remote signals or barrier semaphores. Data moves between devices by JAX's collectives and lax.ppermute only.
A program may use at most 64 MiB of HBM per device.

```python
import math
import jax
import jax.numpy as jnp
from jax import lax

D = 4608
HQ = 32
KVH = 16
HD = 128
FFW = 20480
SLOT = 512
PROMPTS = 8
TOKENS = 4096
N_MP = 32


def draw_lengths(key, part):
    key_short, key_long, key_order = jax.random.split(key, 3)
    count = PROMPTS
    half_count = count // 2
    short_len = jax.random.randint(key_short, (count,), 1, SLOT // 16)
    long_len = jax.random.randint(key_long, (count,), SLOT - SLOT // 8, SLOT + 1)
    slots_idx = jnp.arange(count, dtype=jnp.int32)
    long_len = jnp.where(slots_idx == half_count, SLOT, long_len)
    chosen = jnp.where(slots_idx < half_count, short_len, long_len).astype(jnp.int32)
    order = jax.random.permutation(key_order, count)
    return chosen[order]


def shared_parts(key):
    common_key = jax.random.fold_in(key, 7711)
    key_dir, key_head = jax.random.split(common_key, 2)
    direction = jax.random.rademacher(key_dir, (D,), dtype=jnp.float32)
    head_dirs = jnp.clip(jax.random.normal(key_head, (KVH, HD), jnp.float32), -3.0, 3.0)
    return (direction, head_dirs)


def projection_draw(key, seed_salt, head_count, repeat_count):
    direction, head_dirs = shared_parts(key)
    key_base, key_strength = jax.random.split(jax.random.fold_in(key, seed_salt), 2)
    columns = head_count * HD
    base_part = jnp.clip(jax.random.normal(key_base, (D, columns), jnp.float32), -4.0, 4.0)
    strength = jnp.exp(jax.random.uniform(key_strength, (head_count,), jnp.float32, math.log(0.5), math.log(2.2)))
    per_head = jnp.repeat(head_dirs, repeat_count, axis=0) * strength[:, None]
    weights_all = (base_part + direction[:, None] * per_head.reshape(columns)[None, :]) * (1.0 / math.sqrt(D))
    limit_value = 8.0 / math.sqrt(D)
    return jnp.clip(weights_all, -limit_value, limit_value)


def draw_query_weight(key, part):
    return projection_draw(key, 31, HQ, HQ // KVH)


def draw_key_weight(key, part):
    return projection_draw(key, 37, KVH, 1)


def shard_levels(own_key, shape, pieces, low, top_value):
    loudness, own = 1.0, jax.random.fold_in(own_key, 6)
    for position, blocks in pieces:
        steps = jnp.exp(jax.random.uniform(jax.random.fold_in(own, position), (blocks,), jnp.float32, low / len(pieces), top_value / len(pieces)))
        loudness = loudness * jnp.repeat(steps, shape[position] // blocks).reshape([-1 if axis == position else 1 for axis in range(len(shape))])
    return loudness


def centred(stream_key, dims, scale, most, cuts=(), kind=jnp.bfloat16):
    drawn = jax.random.normal(stream_key, dims, jnp.float32) * scale
    if len(cuts) > 0:
        drawn = shard_levels(stream_key, dims, cuts, -0.22, 0.18) * drawn
    return jnp.clip(drawn, min=-most, max=most).astype(kind)


def setup_inputs(seed: int = 0) -> dict:
    streams_of = jax.random.split(jax.random.key(seed), 12)
    inputs = centred(streams_of[0], (TOKENS, D), 1.0, 6.0, ((0, 256),))
    lengths = draw_lengths(jax.random.fold_in(streams_of[11], 71), 0)
    gain_in = jnp.clip(1.0 + 0.18 * jax.random.normal(streams_of[2], (D,), jnp.float32), 0.1, 1.9)
    query_weight = draw_query_weight(jax.random.fold_in(streams_of[11], 71), 0)
    key_weight = draw_key_weight(jax.random.fold_in(streams_of[11], 71), 0)
    value_weight = centred(streams_of[5], (D, KVH * HD), D ** -0.5, 0.09375, ((0, 8), (1, 32)), jnp.float32)
    output_weight = centred(streams_of[6], (HQ * HD, D), (HQ * HD) ** -0.5, 0.09375, ((0, 32),))
    gain_post = jnp.clip(1.0 + 0.18 * jax.random.normal(streams_of[7], (D,), jnp.float32), 0.1, 1.9)
    gain_pre = jnp.clip(1.0 + 0.18 * jax.random.normal(streams_of[8], (D,), jnp.float32), 0.1, 1.9)
    gate_weight = centred(streams_of[9], (D, FFW), D ** -0.5, 0.09375, ((0, 8), (1, 32)), jnp.float32)
    up_weight = centred(streams_of[10], (D, FFW), D ** -0.5, 0.09375, ((0, 8), (1, 32)), jnp.float32)
    return {"inputs": inputs, "lengths": lengths, "gain_in": gain_in, "query_weight": query_weight, "key_weight": key_weight, "value_weight": value_weight, "output_weight": output_weight, "gain_post": gain_post, "gain_pre": gain_pre, "gate_weight": gate_weight, "up_weight": up_weight}


query_scale = 1.0 / 12.0
soft_cap = 50.0

def rms_norm(values, gain):
    mean_sq = lax.optimization_barrier(jnp.mean(values * values, axis=-1, keepdims=True))
    return values * lax.rsqrt(mean_sq + 1e-06) * gain

def rotate_pairs(values, positions):
    half_size = values.shape[-1] // 2
    freqs = jnp.exp(jnp.arange(half_size, dtype=jnp.float32) * (-2.0 * math.log(10000.0) / values.shape[-1]))
    angles = positions.astype(jnp.float32)[:, None] * freqs[None, :]
    cosine = jnp.cos(angles)[:, None, :]
    sine = jnp.sin(angles)[:, None, :]
    first = values[..., :half_size]
    second = values[..., half_size:]
    return jnp.concatenate([first * cosine - second * sine, second * cosine + first * sine], axis=-1)

def reference(inputs, lengths, gain_in, query_weight, key_weight, value_weight, output_weight, gain_post, gain_pre, gate_weight, up_weight):
    tokens = inputs.shape[0]
    prompts = lengths.shape[0]
    slot = tokens // prompts
    positions = jnp.arange(tokens, dtype=jnp.int32) % slot
    row_len = jnp.repeat(lengths, slot, total_repeat_length=tokens)
    live = positions < row_len
    normed = rms_norm(inputs.astype(jnp.float32), gain_in).astype(jnp.bfloat16)
    raw_q = jnp.dot(normed, query_weight.astype(jnp.bfloat16), preferred_element_type=jnp.float32)
    raw_k = jnp.dot(normed, key_weight.astype(jnp.bfloat16), preferred_element_type=jnp.float32)
    raw_v = jnp.dot(normed, value_weight.astype(jnp.bfloat16), preferred_element_type=jnp.float32)
    queries = rotate_pairs(raw_q.reshape(tokens, HQ, HD), positions).astype(jnp.bfloat16)
    keys_rot = rotate_pairs(raw_k.reshape(tokens, KVH, HD), positions)
    keys_rot = jnp.where(live[:, None, None], keys_rot, jnp.float32(0.0)).astype(jnp.bfloat16)
    values_all = jnp.where(live[:, None], raw_v, jnp.float32(0.0)).astype(jnp.bfloat16).reshape(tokens, KVH, HD)

    def attend(operands):
        query_block, key_block, value_block, length = operands
        key_rep = jnp.repeat(key_block, HQ // KVH, axis=1).astype(jnp.float32)
        value_rep = jnp.repeat(value_block, HQ // KVH, axis=1).astype(jnp.float32)
        scores = jnp.einsum('qhd,khd->hqk', query_block.astype(jnp.float32), key_rep) * query_scale
        capped = soft_cap * jnp.tanh(scores / soft_cap)
        slot_pos = jnp.arange(slot, dtype=jnp.int32)
        allowed = (slot_pos[None, :] <= slot_pos[:, None]) & (slot_pos[None, :] < length)
        weights_exp = jnp.where(allowed[None], jnp.exp(capped), jnp.float32(0.0))
        probs = (weights_exp / lax.optimization_barrier(jnp.sum(weights_exp, axis=-1, keepdims=True))).astype(jnp.bfloat16)
        mixed = jnp.einsum('hqk,khd->qhd', probs.astype(jnp.float32), value_rep)
        mixed = jnp.where((slot_pos < length)[:, None, None], mixed, jnp.float32(0.0))
        return mixed.astype(jnp.bfloat16)
    attended = lax.map(attend, (queries.reshape(prompts, slot, HQ, HD), keys_rot.reshape(prompts, slot, KVH, HD), values_all.reshape(prompts, slot, KVH, HD), lengths))
    attended = attended.reshape(tokens, HQ * HD)
    group_width = HQ * HD // N_MP
    attn = jnp.zeros((tokens, inputs.shape[1]), jnp.float32)
    for group in range(N_MP):
        part_term = jnp.dot(attended[:, group * group_width:(group + 1) * group_width], output_weight[group * group_width:(group + 1) * group_width], preferred_element_type=jnp.float32)
        attn = attn + part_term.astype(jnp.bfloat16).astype(jnp.float32)
    residual = (inputs.astype(jnp.float32) + rms_norm(attn, gain_post)).astype(jnp.bfloat16)
    pre_ffn = rms_norm(residual.astype(jnp.float32), gain_pre).astype(jnp.bfloat16)
    gate = jnp.dot(pre_ffn, gate_weight.astype(jnp.bfloat16), preferred_element_type=jnp.float32)
    up_part = jnp.dot(pre_ffn, up_weight.astype(jnp.bfloat16), preferred_element_type=jnp.float32)
    hidden = (jax.nn.gelu(gate, approximate=True) * up_part).astype(jnp.bfloat16)
    return (residual, hidden, keys_rot.reshape(tokens, KVH * HD), values_all.reshape(tokens, KVH * HD))
```

```python
import math

import jax
import jax.numpy as jnp
from jax import lax
from jax.sharding import PartitionSpec as P

query_scale = 1.0 / 12.0
soft_cap = 50.0


def permute(value, axis, target):
    return lax.ppermute(value, axis, [(k, target(k)) for k in range(lax.axis_size(axis))])


def gather_dp(value):
    count = lax.axis_size("dp")
    index = lax.axis_index("dp")
    partner = permute(value, "dp", lambda k: k ^ 1)
    pieces = [(value, index), (partner, index ^ 1)]
    for step in range(1, count // 2):
        got = permute(value, "dp", lambda k, step=step: (k + 2 * step) % count)
        pieces.append((got, (index - 2 * step) % count))
    for step in range(1, count // 2):
        got = permute(partner, "dp", lambda k, step=step: (k + 2 * step) % count)
        pieces.append((got, ((index - 2 * step) % count) ^ 1))
    stacked = jnp.zeros((count,) + value.shape, value.dtype)
    for piece, where in pieces:
        stacked = lax.dynamic_update_index_in_dim(stacked, piece, where, 0)
    return stacked.reshape(count * value.shape[0], value.shape[1])


def chip_shift(step, chips):
    return lambda k: ((k // 2 + step) % chips) * 2 + k % 2


def gather_mp(value):
    count = lax.axis_size("mp")
    chips = count // 2
    index = lax.axis_index("mp")
    chip = index // 2
    odd = index % 2 == 1
    stacked = jnp.zeros((chips,) + value.shape, value.dtype)
    stacked = lax.dynamic_update_index_in_dim(stacked, value, chip, 0)
    for step in range(1, chips):
        got = permute(value, "mp", chip_shift(step, chips))
        stacked = lax.dynamic_update_index_in_dim(stacked, got, (chip - step) % chips, 0)
    other = permute(stacked, "mp", lambda k: k ^ 1)
    lower = jnp.where(odd, other, stacked)
    upper = jnp.where(odd, stacked, other)
    return jnp.stack([lower, upper], axis=1).reshape(count * value.shape[0], value.shape[1])


def reduce_scatter_mp(value):
    count = lax.axis_size("mp")
    chips = count // 2
    index = lax.axis_index("mp")
    chip = index // 2
    core = index % 2
    rows = value.shape[0] // count
    blocks = value.reshape(chips, 2, rows, value.shape[1])
    mine = lax.dynamic_index_in_dim(blocks, core, 1, keepdims=False)
    theirs = lax.dynamic_index_in_dim(blocks, 1 - core, 1, keepdims=False)
    got = permute(theirs, "mp", lambda k: k ^ 1)
    pair = mine.astype(jnp.float32) + got.astype(jnp.float32)
    pair_bf = pair.astype(jnp.bfloat16)
    total = lax.dynamic_index_in_dim(pair, chip, 0, keepdims=False)
    for step in range(1, chips):
        send = lax.dynamic_index_in_dim(pair_bf, (chip + step) % chips, 0, keepdims=False)
        got = permute(send, "mp", chip_shift(step, chips))
        total = total + got.astype(jnp.float32)
    return total


def rms_norm(values, gain):
    mean_sq = jnp.mean(values * values, axis=-1, keepdims=True)
    return values * lax.rsqrt(mean_sq + 1e-06) * gain


def rotate_pairs(values, positions):
    half_size = values.shape[-1] // 2
    freqs = jnp.exp(
        jnp.arange(half_size, dtype=jnp.float32) * (-2.0 * math.log(10000.0) / values.shape[-1])
    )
    angles = positions.astype(jnp.float32)[:, None] * freqs[None, :]
    cosine = jnp.cos(angles)[:, None, :]
    sine = jnp.sin(angles)[:, None, :]
    first = values[..., :half_size]
    second = values[..., half_size:]
    return jnp.concatenate(
        [first * cosine - second * sine, second * cosine + first * sine], axis=-1
    )


def join_halves(own_half, other_half, odd_flag):
    lower_first = jnp.concatenate([own_half, other_half], axis=1)
    upper_first = jnp.concatenate([other_half, own_half], axis=1)
    return jnp.where(odd_flag, upper_first, lower_first)


def head_block(query_rows, key_rows, value_rows, key_count, length):
    scores = (
        jnp.einsum("qhd,kd->hqk", query_rows, key_rows, preferred_element_type=jnp.float32)
        * query_scale
    )
    capped = soft_cap * jnp.tanh(scores / soft_cap)
    query_pos = jnp.arange(query_rows.shape[0], dtype=jnp.int32)
    key_pos = jnp.arange(key_count, dtype=jnp.int32)
    allowed = (key_pos[None, :] <= query_pos[:, None]) & (key_pos[None, :] < length)
    weights_exp = jnp.where(allowed[None], jnp.exp(capped), jnp.float32(0.0))
    probs = (weights_exp / jnp.sum(weights_exp, axis=-1, keepdims=True)).astype(jnp.bfloat16)
    return jnp.einsum("hqk,kd->qhd", probs, value_rows, preferred_element_type=jnp.float32)


def on_device(
    inputs,
    lengths,
    gain_in,
    query_weight,
    key_weight,
    value_weight,
    output_weight,
    gain_post,
    gain_pre,
    gate_weight,
    up_weight,
):
    mp_index = lax.axis_index("mp")
    odd_flag = mp_index % 2 == 1
    query_width = query_weight.shape[1]
    own_width = key_weight.shape[1]
    ffn_width = gate_weight.shape[1]
    qkv_own = jnp.concatenate(
        [query_weight, key_weight, value_weight], axis=1
    ).astype(jnp.bfloat16)
    ffn_own = jnp.concatenate([gate_weight, up_weight], axis=1).astype(jnp.bfloat16)
    qkv_full = gather_dp(qkv_own)
    ffn_full = gather_dp(ffn_own)

    normed_local = rms_norm(inputs.astype(jnp.float32), gain_in).astype(jnp.bfloat16)
    normed = gather_mp(normed_local)
    group_tokens = normed.shape[0]
    slot = group_tokens

    raw = jnp.dot(normed, qkv_full, preferred_element_type=jnp.float32)
    raw_q = raw[:, :query_width]
    raw_kv_own = raw[:, query_width:]
    raw_kv_other = permute(raw_kv_own, "mp", lambda k: k ^ 1)
    raw_k = join_halves(raw_kv_own[:, :own_width], raw_kv_other[:, :own_width], odd_flag)
    raw_v = join_halves(raw_kv_own[:, own_width:], raw_kv_other[:, own_width:], odd_flag)

    head_size = raw_k.shape[1]
    local_heads = raw_q.shape[1] // head_size
    positions = jnp.arange(group_tokens, dtype=jnp.int32)
    length = lengths[0]
    live = positions < length
    queries = rotate_pairs(raw_q.reshape(group_tokens, local_heads, head_size), positions).astype(
        jnp.bfloat16
    )
    keys_rot = rotate_pairs(raw_k.reshape(group_tokens, 1, head_size), positions).reshape(
        group_tokens, head_size
    )
    keys_rot = jnp.where(live[:, None], keys_rot, jnp.float32(0.0)).astype(jnp.bfloat16)
    values_all = jnp.where(live[:, None], raw_v, jnp.float32(0.0)).astype(jnp.bfloat16)
    mixed = head_block(queries, keys_rot, values_all, slot, length)
    mixed = jnp.where(live[:, None, None], mixed, jnp.float32(0.0))
    attended = mixed.astype(jnp.bfloat16).reshape(slot, local_heads * head_size)
    partial = jnp.dot(attended, output_weight, preferred_element_type=jnp.float32).astype(
        jnp.bfloat16
    )
    attn_rows = reduce_scatter_mp(partial)
    residual = (inputs.astype(jnp.float32) + rms_norm(attn_rows, gain_post)).astype(jnp.bfloat16)
    pre_local = rms_norm(residual.astype(jnp.float32), gain_pre).astype(jnp.bfloat16)
    pre_ffn = gather_mp(pre_local)
    both = jnp.dot(pre_ffn, ffn_full, preferred_element_type=jnp.float32)
    gate = both[:, :ffn_width]
    up_part = both[:, ffn_width:]
    hidden = (jax.nn.gelu(gate, approximate=True) * up_part).astype(jnp.bfloat16)
    offset = mp_index % 2 * own_width
    keys_out = lax.dynamic_slice_in_dim(keys_rot, offset, own_width, 1)
    values_out = lax.dynamic_slice_in_dim(values_all, offset, own_width, 1)
    return (residual, hidden, keys_out, values_out)


def solution(mesh):
    in_specs = (
        P(("dp", "mp"), None),
        P("dp"),
        P(),
        P("dp", "mp"),
        P("dp", "mp"),
        P("dp", "mp"),
        P("mp", None),
        P(),
        P(),
        P("dp", "mp"),
        P("dp", "mp"),
    )
    out_specs = (P(("dp", "mp"), None), P("dp", "mp"), P("dp", "mp"), P("dp", "mp"))
    return jax.shard_map(
        on_device, mesh=mesh, in_specs=in_specs, out_specs=out_specs, check_vma=False
    )
```

```python
import math

import jax
import jax.numpy as jnp
from jax import lax
from jax.sharding import PartitionSpec as P

query_scale = 1.0 / 12.0
soft_cap = 50.0


def permute(value, axis, target):
    return lax.ppermute(value, axis, [(k, target(k)) for k in range(lax.axis_size(axis))])


def gather_dp(value):
    count = lax.axis_size("dp")
    index = lax.axis_index("dp")
    partner = permute(value, "dp", lambda k: k ^ 1)
    pieces = [(value, index), (partner, index ^ 1)]
    for step in range(1, count // 2):
        got = permute(value, "dp", lambda k, step=step: (k + 2 * step) % count)
        pieces.append((got, (index - 2 * step) % count))
    for step in range(1, count // 2):
        got = permute(partner, "dp", lambda k, step=step: (k + 2 * step) % count)
        pieces.append((got, ((index - 2 * step) % count) ^ 1))
    stacked = jnp.zeros((count,) + value.shape, value.dtype)
    for piece, where in pieces:
        stacked = lax.dynamic_update_index_in_dim(stacked, piece, where, 0)
    return stacked.reshape(count * value.shape[0], value.shape[1])


def pair_order(value, other, low_flag, axis):
    lower = jnp.where(low_flag, value, other)
    upper = jnp.where(low_flag, other, value)
    return jnp.stack([lower, upper], axis=axis)


def gather_mp(value):
    count = lax.axis_size("mp")
    index = lax.axis_index("mp")
    chip_bits = (count // 2).bit_length() - 1
    order = [1, 3, 0, 2] if chip_bits == 4 else list(range(chip_bits))
    held = []
    stacked = value
    for bit in order:
        other = permute(stacked, "mp", lambda k, bit=bit: k ^ (2 << bit))
        low_flag = (index >> (bit + 1)) % 2 == 0
        position = sum(1 for b in held if b > bit)
        stacked = pair_order(stacked, other, low_flag, position)
        held.append(bit)
    other = permute(stacked, "mp", lambda k: k ^ 1)
    stacked = pair_order(stacked, other, index % 2 == 0, chip_bits)
    return stacked.reshape(count * value.shape[0], value.shape[1])


def reduce_scatter_mp(value):
    count = lax.axis_size("mp")
    index = lax.axis_index("mp")
    chip_bits = (count // 2).bit_length() - 1
    rows = value.shape[0] // count
    blocks = value.reshape([2] * chip_bits + [2, rows, value.shape[1]])
    core = index % 2
    mine = lax.dynamic_index_in_dim(blocks, core, chip_bits, keepdims=False)
    theirs = lax.dynamic_index_in_dim(blocks, 1 - core, chip_bits, keepdims=False)
    got = permute(theirs, "mp", lambda k: k ^ 1)
    total = mine.astype(jnp.float32) + got.astype(jnp.float32)
    held = list(range(chip_bits - 1, -1, -1))
    order = [2, 0, 3, 1] if chip_bits == 4 else list(range(chip_bits))
    for bit in order:
        axis = held.index(bit)
        mine_bit = (index >> (bit + 1)) % 2
        keep = lax.dynamic_index_in_dim(total, mine_bit, axis, keepdims=False)
        send = lax.dynamic_index_in_dim(total, 1 - mine_bit, axis, keepdims=False)
        got = permute(send.astype(jnp.bfloat16), "mp", lambda k, bit=bit: k ^ (2 << bit))
        total = keep + got.astype(jnp.float32)
        held.remove(bit)
    return total


def rms_norm(values, gain):
    mean_sq = jnp.mean(values * values, axis=-1, keepdims=True)
    return values * lax.rsqrt(mean_sq + 1e-06) * gain


def rotate_pairs(values, positions):
    half_size = values.shape[-1] // 2
    freqs = jnp.exp(
        jnp.arange(half_size, dtype=jnp.float32) * (-2.0 * math.log(10000.0) / values.shape[-1])
    )
    angles = positions.astype(jnp.float32)[:, None] * freqs[None, :]
    cosine = jnp.cos(angles)[:, None, :]
    sine = jnp.sin(angles)[:, None, :]
    first = values[..., :half_size]
    second = values[..., half_size:]
    return jnp.concatenate(
        [first * cosine - second * sine, second * cosine + first * sine], axis=-1
    )


def join_halves(own_half, other_half, odd_flag):
    lower_first = jnp.concatenate([own_half, other_half], axis=1)
    upper_first = jnp.concatenate([other_half, own_half], axis=1)
    return jnp.where(odd_flag, upper_first, lower_first)


def head_block(query_rows, key_rows, value_rows, key_count, length):
    scores = (
        jnp.einsum("qhd,kd->hqk", query_rows, key_rows, preferred_element_type=jnp.float32)
        * query_scale
    )
    capped = soft_cap * jnp.tanh(scores / soft_cap)
    query_pos = jnp.arange(query_rows.shape[0], dtype=jnp.int32)
    key_pos = jnp.arange(key_count, dtype=jnp.int32)
    allowed = (key_pos[None, :] <= query_pos[:, None]) & (key_pos[None, :] < length)
    weights_exp = jnp.where(allowed[None], jnp.exp(capped), jnp.float32(0.0))
    probs = (weights_exp / jnp.sum(weights_exp, axis=-1, keepdims=True)).astype(jnp.bfloat16)
    return jnp.einsum("hqk,kd->qhd", probs, value_rows, preferred_element_type=jnp.float32)


def on_device(
    inputs,
    lengths,
    gain_in,
    query_weight,
    key_weight,
    value_weight,
    output_weight,
    gain_post,
    gain_pre,
    gate_weight,
    up_weight,
):
    mp_index = lax.axis_index("mp")
    odd_flag = mp_index % 2 == 1
    query_width = query_weight.shape[1]
    own_width = key_weight.shape[1]
    ffn_width = gate_weight.shape[1]
    qkv_own = jnp.concatenate(
        [query_weight, key_weight, value_weight], axis=1
    ).astype(jnp.bfloat16)
    ffn_own = jnp.concatenate([gate_weight, up_weight], axis=1).astype(jnp.bfloat16)
    qkv_full = gather_dp(qkv_own)
    ffn_full = gather_dp(ffn_own)

    normed_local = rms_norm(inputs.astype(jnp.float32), gain_in).astype(jnp.bfloat16)
    normed = gather_mp(normed_local)
    group_tokens = normed.shape[0]
    slot = group_tokens

    raw = jnp.dot(normed, qkv_full, preferred_element_type=jnp.float32)
    raw_q = raw[:, :query_width]
    raw_kv_own = raw[:, query_width:]
    raw_kv_other = permute(raw_kv_own, "mp", lambda k: k ^ 1)
    raw_k = join_halves(raw_kv_own[:, :own_width], raw_kv_other[:, :own_width], odd_flag)
    raw_v = join_halves(raw_kv_own[:, own_width:], raw_kv_other[:, own_width:], odd_flag)

    head_size = raw_k.shape[1]
    local_heads = raw_q.shape[1] // head_size
    positions = jnp.arange(group_tokens, dtype=jnp.int32)
    length = lengths[0]
    live = positions < length
    queries = rotate_pairs(raw_q.reshape(group_tokens, local_heads, head_size), positions).astype(
        jnp.bfloat16
    )
    keys_rot = rotate_pairs(raw_k.reshape(group_tokens, 1, head_size), positions).reshape(
        group_tokens, head_size
    )
    keys_rot = jnp.where(live[:, None], keys_rot, jnp.float32(0.0)).astype(jnp.bfloat16)
    values_all = jnp.where(live[:, None], raw_v, jnp.float32(0.0)).astype(jnp.bfloat16)
    mixed = head_block(queries, keys_rot, values_all, slot, length)
    mixed = jnp.where(live[:, None, None], mixed, jnp.float32(0.0))
    attended = mixed.astype(jnp.bfloat16).reshape(slot, local_heads * head_size)
    partial = jnp.dot(attended, output_weight, preferred_element_type=jnp.float32).astype(
        jnp.bfloat16
    )
    attn_rows = reduce_scatter_mp(partial)
    ffn_full, attn_rows = lax.optimization_barrier((ffn_full, attn_rows))
    residual = (inputs.astype(jnp.float32) + rms_norm(attn_rows, gain_post)).astype(jnp.bfloat16)
    pre_local = rms_norm(residual.astype(jnp.float32), gain_pre).astype(jnp.bfloat16)
    pre_ffn = gather_mp(pre_local)
    both = jnp.dot(pre_ffn, ffn_full, preferred_element_type=jnp.float32)
    gate = both[:, :ffn_width]
    up_part = both[:, ffn_width:]
    hidden = (jax.nn.gelu(gate, approximate=True) * up_part).astype(jnp.bfloat16)
    offset = mp_index % 2 * own_width
    keys_out = lax.dynamic_slice_in_dim(keys_rot, offset, own_width, 1)
    values_out = lax.dynamic_slice_in_dim(values_all, offset, own_width, 1)
    return (residual, hidden, keys_out, values_out)


def solution(mesh):
    in_specs = (
        P(("dp", "mp"), None),
        P("dp"),
        P(),
        P("dp", "mp"),
        P("dp", "mp"),
        P("dp", "mp"),
        P("mp", None),
        P(),
        P(),
        P("dp", "mp"),
        P("dp", "mp"),
    )
    out_specs = (P(("dp", "mp"), None), P("dp", "mp"), P("dp", "mp"), P("dp", "mp"))
    return jax.shard_map(
        on_device, mesh=mesh, in_specs=in_specs, out_specs=out_specs, check_vma=False
    )
```

```python
import math

import jax
import jax.numpy as jnp
from jax import lax
from jax.sharding import PartitionSpec as P

query_scale = 1.0 / 12.0
soft_cap = 50.0


def permute(value, axis, target):
    return lax.ppermute(value, axis, [(k, target(k)) for k in range(lax.axis_size(axis))])


def gather_dp(value, partner=None):
    count = lax.axis_size("dp")
    index = lax.axis_index("dp")
    if partner is None:
        partner = permute(value, "dp", lambda k: k ^ 1)
    pieces = [(value, index), (partner, index ^ 1)]
    for step in range(1, count // 2):
        got = permute(value, "dp", lambda k, step=step: (k + 2 * step) % count)
        pieces.append((got, (index - 2 * step) % count))
    for step in range(1, count // 2):
        got = permute(partner, "dp", lambda k, step=step: (k + 2 * step) % count)
        pieces.append((got, ((index - 2 * step) % count) ^ 1))
    stacked = jnp.zeros((count,) + value.shape, value.dtype)
    for piece, where in pieces:
        stacked = lax.dynamic_update_index_in_dim(stacked, piece, where, 0)
    return stacked.reshape(count * value.shape[0], value.shape[1])


def pair_order(value, other, low_flag, axis):
    lower = jnp.where(low_flag, value, other)
    upper = jnp.where(low_flag, other, value)
    return jnp.stack([lower, upper], axis=axis)


def chip_orders(chip_bits):
    if chip_bits == 4:
        return [1, 3, 0, 2], [3, 1, 2, 0]
    return list(range(chip_bits)), list(range(chip_bits))


def bit_by_core(index, even_bits, odd_bits, step):
    return jnp.where(index % 2 == 0, even_bits[step], odd_bits[step])


def step_partner(even_bit, odd_bit):
    return lambda k: k ^ (2 << (even_bit if k % 2 == 0 else odd_bit))


def to_bit_order(stacked, axis_bits, chip_bits):
    return stacked.transpose([axis_bits.index(b) for b in range(chip_bits - 1, -1, -1)] + list(range(chip_bits, stacked.ndim)))


def gather_mp(value):
    count = lax.axis_size("mp")
    index = lax.axis_index("mp")
    chip_bits = (count // 2).bit_length() - 1
    even_bits, odd_bits = chip_orders(chip_bits)
    stacked = value
    for step in range(chip_bits):
        other = permute(stacked, "mp", step_partner(even_bits[step], odd_bits[step]))
        bit = bit_by_core(index, even_bits, odd_bits, step)
        stacked = pair_order(stacked, other, (index >> (bit + 1)) % 2 == 0, 0)
    even_axes = list(reversed(even_bits))
    odd_axes = list(reversed(odd_bits))
    stacked = jnp.where(
        index % 2 == 0,
        to_bit_order(stacked, even_axes, chip_bits),
        to_bit_order(stacked, odd_axes, chip_bits),
    )
    other = permute(stacked, "mp", lambda k: k ^ 1)
    stacked = pair_order(stacked, other, index % 2 == 0, chip_bits)
    return stacked.reshape(count * value.shape[0], value.shape[1])


def from_bit_order(blocks, step_bits, chip_bits):
    return blocks.transpose([chip_bits - 1 - b for b in step_bits] + list(range(chip_bits, blocks.ndim)))


def reduce_scatter_mp(value):
    count = lax.axis_size("mp")
    index = lax.axis_index("mp")
    chip_bits = (count // 2).bit_length() - 1
    rows = value.shape[0] // count
    even_bits, odd_bits = chip_orders(chip_bits)
    even_bits, odd_bits = even_bits[::-1], odd_bits[::-1]
    blocks = value.reshape([2] * chip_bits + [2, rows, value.shape[1]])
    core = index % 2
    mine = lax.dynamic_index_in_dim(blocks, core, chip_bits, keepdims=False)
    theirs = lax.dynamic_index_in_dim(blocks, 1 - core, chip_bits, keepdims=False)
    got = permute(theirs, "mp", lambda k: k ^ 1)
    total = mine.astype(jnp.float32) + got.astype(jnp.float32)
    total = jnp.where(
        index % 2 == 0,
        from_bit_order(total, even_bits, chip_bits),
        from_bit_order(total, odd_bits, chip_bits),
    )
    for step in range(chip_bits):
        bit = bit_by_core(index, even_bits, odd_bits, step)
        mine_bit = (index >> (bit + 1)) % 2
        keep = lax.dynamic_index_in_dim(total, mine_bit, 0, keepdims=False)
        send = lax.dynamic_index_in_dim(total, 1 - mine_bit, 0, keepdims=False)
        got = permute(
            send.astype(jnp.bfloat16), "mp", step_partner(even_bits[step], odd_bits[step])
        )
        total = keep + got.astype(jnp.float32)
    return total


def rms_norm(values, gain):
    mean_sq = jnp.mean(values * values, axis=-1, keepdims=True)
    return values * lax.rsqrt(mean_sq + 1e-06) * gain


def rotate_pairs(values, positions):
    half_size = values.shape[-1] // 2
    freqs = jnp.exp(
        jnp.arange(half_size, dtype=jnp.float32) * (-2.0 * math.log(10000.0) / values.shape[-1])
    )
    angles = positions.astype(jnp.float32)[:, None] * freqs[None, :]
    cosine = jnp.cos(angles)[:, None, :]
    sine = jnp.sin(angles)[:, None, :]
    first = values[..., :half_size]
    second = values[..., half_size:]
    return jnp.concatenate(
        [first * cosine - second * sine, second * cosine + first * sine], axis=-1
    )


def join_halves(own_half, other_half, odd_flag):
    lower_first = jnp.concatenate([own_half, other_half], axis=1)
    upper_first = jnp.concatenate([other_half, own_half], axis=1)
    return jnp.where(odd_flag, upper_first, lower_first)


def head_block(query_rows, key_rows, value_rows, key_count, length):
    scores = (
        jnp.einsum("qhd,kd->hqk", query_rows, key_rows, preferred_element_type=jnp.float32)
        * query_scale
    )
    capped = soft_cap * jnp.tanh(scores / soft_cap)
    query_pos = jnp.arange(query_rows.shape[0], dtype=jnp.int32)
    key_pos = jnp.arange(key_count, dtype=jnp.int32)
    allowed = (key_pos[None, :] <= query_pos[:, None]) & (key_pos[None, :] < length)
    weights_exp = jnp.where(allowed[None], jnp.exp(capped), jnp.float32(0.0))
    probs = (weights_exp / jnp.sum(weights_exp, axis=-1, keepdims=True)).astype(jnp.bfloat16)
    return jnp.einsum("hqk,kd->qhd", probs, value_rows, preferred_element_type=jnp.float32)


def on_device(
    inputs,
    lengths,
    gain_in,
    query_weight,
    key_weight,
    value_weight,
    output_weight,
    gain_post,
    gain_pre,
    gate_weight,
    up_weight,
):
    mp_index = lax.axis_index("mp")
    odd_flag = mp_index % 2 == 1
    query_width = query_weight.shape[1]
    own_width = key_weight.shape[1]
    ffn_width = gate_weight.shape[1]
    qkv_own = jnp.concatenate(
        [query_weight, key_weight, value_weight], axis=1
    ).astype(jnp.bfloat16)
    ffn_own = jnp.concatenate([gate_weight, up_weight], axis=1).astype(jnp.bfloat16)
    qkv_full = gather_dp(qkv_own)
    ffn_partner = permute(ffn_own, "dp", lambda k: k ^ 1)

    normed_local = rms_norm(inputs.astype(jnp.float32), gain_in).astype(jnp.bfloat16)
    normed = gather_mp(normed_local)
    group_tokens = normed.shape[0]
    slot = group_tokens

    raw = jnp.dot(normed, qkv_full, preferred_element_type=jnp.float32)
    raw_q = raw[:, :query_width]
    raw_kv_own = raw[:, query_width:]
    raw_kv_other = permute(raw_kv_own, "mp", lambda k: k ^ 1)
    raw_k = join_halves(raw_kv_own[:, :own_width], raw_kv_other[:, :own_width], odd_flag)
    raw_v = join_halves(raw_kv_own[:, own_width:], raw_kv_other[:, own_width:], odd_flag)

    head_size = raw_k.shape[1]
    local_heads = raw_q.shape[1] // head_size
    positions = jnp.arange(group_tokens, dtype=jnp.int32)
    length = lengths[0]
    live = positions < length
    queries = rotate_pairs(raw_q.reshape(group_tokens, local_heads, head_size), positions).astype(
        jnp.bfloat16
    )
    keys_rot = rotate_pairs(raw_k.reshape(group_tokens, 1, head_size), positions).reshape(
        group_tokens, head_size
    )
    keys_rot = jnp.where(live[:, None], keys_rot, jnp.float32(0.0)).astype(jnp.bfloat16)
    values_all = jnp.where(live[:, None], raw_v, jnp.float32(0.0)).astype(jnp.bfloat16)
    mixed = head_block(queries, keys_rot, values_all, slot, length)
    mixed = jnp.where(live[:, None, None], mixed, jnp.float32(0.0))
    attended = mixed.astype(jnp.bfloat16).reshape(slot, local_heads * head_size)
    partial = jnp.dot(attended, output_weight, preferred_element_type=jnp.float32).astype(
        jnp.bfloat16
    )
    ffn_partner, partial = lax.optimization_barrier((ffn_partner, partial))
    ffn_full = gather_dp(ffn_own, ffn_partner)
    attn_rows = reduce_scatter_mp(partial)
    ffn_full, attn_rows = lax.optimization_barrier((ffn_full, attn_rows))
    residual = (inputs.astype(jnp.float32) + rms_norm(attn_rows, gain_post)).astype(jnp.bfloat16)
    pre_local = rms_norm(residual.astype(jnp.float32), gain_pre).astype(jnp.bfloat16)
    pre_ffn = gather_mp(pre_local)
    both = jnp.dot(pre_ffn, ffn_full, preferred_element_type=jnp.float32)
    gate = both[:, :ffn_width]
    up_part = both[:, ffn_width:]
    hidden = (jax.nn.gelu(gate, approximate=True) * up_part).astype(jnp.bfloat16)
    offset = mp_index % 2 * own_width
    keys_out = lax.dynamic_slice_in_dim(keys_rot, offset, own_width, 1)
    values_out = lax.dynamic_slice_in_dim(values_all, offset, own_width, 1)
    return (residual, hidden, keys_out, values_out)


def solution(mesh):
    in_specs = (
        P(("dp", "mp"), None),
        P("dp"),
        P(),
        P("dp", "mp"),
        P("dp", "mp"),
        P("dp", "mp"),
        P("mp", None),
        P(),
        P(),
        P("dp", "mp"),
        P("dp", "mp"),
    )
    out_specs = (P(("dp", "mp"), None), P("dp", "mp"), P("dp", "mp"), P("dp", "mp"))
    return jax.shard_map(
        on_device, mesh=mesh, in_specs=in_specs, out_specs=out_specs, check_vma=False
    )
```

```python
import math

import jax
import jax.numpy as jnp
from jax import lax
from jax.sharding import PartitionSpec as P

query_scale = 1.0 / 12.0
soft_cap = 50.0


def permute(value, axis, target):
    return lax.ppermute(value, axis, [(k, target(k)) for k in range(lax.axis_size(axis))])


def gather_dp(value, partner=None):
    count = lax.axis_size("dp")
    index = lax.axis_index("dp")
    if partner is None:
        partner = permute(value, "dp", lambda k: k ^ 1)
    if count != 8:
        return gather_dp_direct(value, partner)
    half = value.shape[0] // 2
    up = lambda k: (k + 2) % count
    down = lambda k: (k - 2) % count
    from_below = permute(value, "dp", up)
    from_above = permute(value, "dp", down)
    partner_below = permute(partner, "dp", up)
    partner_above = permute(partner, "dp", down)
    far_low = permute(from_below[:half], "dp", up)
    far_high = permute(from_above[half:], "dp", down)
    far_partner_low = permute(partner_below[:half], "dp", up)
    far_partner_high = permute(partner_above[half:], "dp", down)
    pieces = [
        (value, index),
        (partner, index ^ 1),
        (from_below, (index - 2) % count),
        (from_above, (index + 2) % count),
        (partner_below, ((index - 2) % count) ^ 1),
        (partner_above, ((index + 2) % count) ^ 1),
        (jnp.concatenate([far_low, far_high]), (index + 4) % count),
        (jnp.concatenate([far_partner_low, far_partner_high]), ((index + 4) % count) ^ 1),
    ]
    stacked = jnp.zeros((count,) + value.shape, value.dtype)
    for piece, where in pieces:
        stacked = lax.dynamic_update_index_in_dim(stacked, piece, where, 0)
    return stacked.reshape(count * value.shape[0], value.shape[1])


def gather_dp_direct(value, partner):
    count = lax.axis_size("dp")
    index = lax.axis_index("dp")
    pieces = [(value, index), (partner, index ^ 1)]
    for step in range(1, count // 2):
        got = permute(value, "dp", lambda k, step=step: (k + 2 * step) % count)
        pieces.append((got, (index - 2 * step) % count))
    for step in range(1, count // 2):
        got = permute(partner, "dp", lambda k, step=step: (k + 2 * step) % count)
        pieces.append((got, ((index - 2 * step) % count) ^ 1))
    stacked = jnp.zeros((count,) + value.shape, value.dtype)
    for piece, where in pieces:
        stacked = lax.dynamic_update_index_in_dim(stacked, piece, where, 0)
    return stacked.reshape(count * value.shape[0], value.shape[1])


def pair_order(value, other, low_flag, axis):
    lower = jnp.where(low_flag, value, other)
    upper = jnp.where(low_flag, other, value)
    return jnp.stack([lower, upper], axis=axis)


def chip_orders(chip_bits):
    if chip_bits == 4:
        return [1, 3, 0, 2], [3, 1, 2, 0]
    return list(range(chip_bits)), list(range(chip_bits))


def bit_by_core(index, even_bits, odd_bits, step):
    return jnp.where(index % 2 == 0, even_bits[step], odd_bits[step])


def step_partner(even_bit, odd_bit):
    return lambda k: k ^ (2 << (even_bit if k % 2 == 0 else odd_bit))


def to_bit_order(stacked, axis_bits, chip_bits):
    return stacked.transpose([axis_bits.index(b) for b in range(chip_bits - 1, -1, -1)] + list(range(chip_bits, stacked.ndim)))


def gather_mp(value):
    count = lax.axis_size("mp")
    index = lax.axis_index("mp")
    chip_bits = (count // 2).bit_length() - 1
    even_bits, odd_bits = chip_orders(chip_bits)
    stacked = value
    for step in range(chip_bits):
        other = permute(stacked, "mp", step_partner(even_bits[step], odd_bits[step]))
        bit = bit_by_core(index, even_bits, odd_bits, step)
        stacked = pair_order(stacked, other, (index >> (bit + 1)) % 2 == 0, 0)
    even_axes = list(reversed(even_bits))
    odd_axes = list(reversed(odd_bits))
    stacked = jnp.where(
        index % 2 == 0,
        to_bit_order(stacked, even_axes, chip_bits),
        to_bit_order(stacked, odd_axes, chip_bits),
    )
    other = permute(stacked, "mp", lambda k: k ^ 1)
    stacked = pair_order(stacked, other, index % 2 == 0, chip_bits)
    return stacked.reshape(count * value.shape[0], value.shape[1])


def from_bit_order(blocks, step_bits, chip_bits):
    return blocks.transpose([chip_bits - 1 - b for b in step_bits] + list(range(chip_bits, blocks.ndim)))


def reduce_scatter_mp(value):
    count = lax.axis_size("mp")
    index = lax.axis_index("mp")
    chip_bits = (count // 2).bit_length() - 1
    rows = value.shape[0] // count
    even_bits, odd_bits = chip_orders(chip_bits)
    even_bits, odd_bits = even_bits[::-1], odd_bits[::-1]
    blocks = value.reshape([2] * chip_bits + [2, rows, value.shape[1]])
    core = index % 2
    mine = lax.dynamic_index_in_dim(blocks, core, chip_bits, keepdims=False)
    theirs = lax.dynamic_index_in_dim(blocks, 1 - core, chip_bits, keepdims=False)
    got = permute(theirs, "mp", lambda k: k ^ 1)
    total = mine.astype(jnp.float32) + got.astype(jnp.float32)
    total = jnp.where(
        index % 2 == 0,
        from_bit_order(total, even_bits, chip_bits),
        from_bit_order(total, odd_bits, chip_bits),
    )
    for step in range(chip_bits):
        bit = bit_by_core(index, even_bits, odd_bits, step)
        mine_bit = (index >> (bit + 1)) % 2
        keep = lax.dynamic_index_in_dim(total, mine_bit, 0, keepdims=False)
        send = lax.dynamic_index_in_dim(total, 1 - mine_bit, 0, keepdims=False)
        got = permute(
            send.astype(jnp.bfloat16), "mp", step_partner(even_bits[step], odd_bits[step])
        )
        total = keep + got.astype(jnp.float32)
    return total


def rms_norm(values, gain):
    mean_sq = jnp.mean(values * values, axis=-1, keepdims=True)
    return values * lax.rsqrt(mean_sq + 1e-06) * gain


def rotate_pairs(values, positions):
    half_size = values.shape[-1] // 2
    freqs = jnp.exp(
        jnp.arange(half_size, dtype=jnp.float32) * (-2.0 * math.log(10000.0) / values.shape[-1])
    )
    angles = positions.astype(jnp.float32)[:, None] * freqs[None, :]
    cosine = jnp.cos(angles)[:, None, :]
    sine = jnp.sin(angles)[:, None, :]
    first = values[..., :half_size]
    second = values[..., half_size:]
    return jnp.concatenate(
        [first * cosine - second * sine, second * cosine + first * sine], axis=-1
    )


def join_halves(own_half, other_half, odd_flag):
    lower_first = jnp.concatenate([own_half, other_half], axis=1)
    upper_first = jnp.concatenate([other_half, own_half], axis=1)
    return jnp.where(odd_flag, upper_first, lower_first)


def head_block(query_rows, key_rows, value_rows, key_count, length):
    scores = (
        jnp.einsum("qhd,kd->hqk", query_rows, key_rows, preferred_element_type=jnp.float32)
        * query_scale
    )
    capped = soft_cap * jnp.tanh(scores / soft_cap)
    query_pos = jnp.arange(query_rows.shape[0], dtype=jnp.int32)
    key_pos = jnp.arange(key_count, dtype=jnp.int32)
    allowed = (key_pos[None, :] <= query_pos[:, None]) & (key_pos[None, :] < length)
    weights_exp = jnp.where(allowed[None], jnp.exp(capped), jnp.float32(0.0))
    probs = (weights_exp / jnp.sum(weights_exp, axis=-1, keepdims=True)).astype(jnp.bfloat16)
    return jnp.einsum("hqk,kd->qhd", probs, value_rows, preferred_element_type=jnp.float32)


def on_device(
    inputs,
    lengths,
    gain_in,
    query_weight,
    key_weight,
    value_weight,
    output_weight,
    gain_post,
    gain_pre,
    gate_weight,
    up_weight,
):
    mp_index = lax.axis_index("mp")
    odd_flag = mp_index % 2 == 1
    query_width = query_weight.shape[1]
    own_width = key_weight.shape[1]
    ffn_width = gate_weight.shape[1]
    qkv_own = jnp.concatenate(
        [query_weight, key_weight, value_weight], axis=1
    ).astype(jnp.bfloat16)
    ffn_own = jnp.concatenate([gate_weight, up_weight], axis=1).astype(jnp.bfloat16)
    qkv_full = gather_dp(qkv_own)
    ffn_partner = permute(ffn_own, "dp", lambda k: k ^ 1)

    normed_local = rms_norm(inputs.astype(jnp.float32), gain_in).astype(jnp.bfloat16)
    normed = gather_mp(normed_local)
    group_tokens = normed.shape[0]
    slot = group_tokens

    raw = jnp.dot(normed, qkv_full, preferred_element_type=jnp.float32)
    raw_q = raw[:, :query_width]
    raw_kv_own = raw[:, query_width:]
    raw_kv_other = permute(raw_kv_own, "mp", lambda k: k ^ 1)
    raw_k = join_halves(raw_kv_own[:, :own_width], raw_kv_other[:, :own_width], odd_flag)
    raw_v = join_halves(raw_kv_own[:, own_width:], raw_kv_other[:, own_width:], odd_flag)

    head_size = raw_k.shape[1]
    local_heads = raw_q.shape[1] // head_size
    positions = jnp.arange(group_tokens, dtype=jnp.int32)
    length = lengths[0]
    live = positions < length
    queries = rotate_pairs(raw_q.reshape(group_tokens, local_heads, head_size), positions).astype(
        jnp.bfloat16
    )
    keys_rot = rotate_pairs(raw_k.reshape(group_tokens, 1, head_size), positions).reshape(
        group_tokens, head_size
    )
    keys_rot = jnp.where(live[:, None], keys_rot, jnp.float32(0.0)).astype(jnp.bfloat16)
    values_all = jnp.where(live[:, None], raw_v, jnp.float32(0.0)).astype(jnp.bfloat16)
    mixed = head_block(queries, keys_rot, values_all, slot, length)
    mixed = jnp.where(live[:, None, None], mixed, jnp.float32(0.0))
    attended = mixed.astype(jnp.bfloat16).reshape(slot, local_heads * head_size)
    partial = jnp.dot(attended, output_weight, preferred_element_type=jnp.float32).astype(
        jnp.bfloat16
    )
    ffn_partner, partial = lax.optimization_barrier((ffn_partner, partial))
    ffn_full = gather_dp(ffn_own, ffn_partner)
    attn_rows = reduce_scatter_mp(partial)
    ffn_full, attn_rows = lax.optimization_barrier((ffn_full, attn_rows))
    residual = (inputs.astype(jnp.float32) + rms_norm(attn_rows, gain_post)).astype(jnp.bfloat16)
    pre_local = rms_norm(residual.astype(jnp.float32), gain_pre).astype(jnp.bfloat16)
    pre_ffn = gather_mp(pre_local)
    both = jnp.dot(pre_ffn, ffn_full, preferred_element_type=jnp.float32)
    gate = both[:, :ffn_width]
    up_part = both[:, ffn_width:]
    hidden = (jax.nn.gelu(gate, approximate=True) * up_part).astype(jnp.bfloat16)
    offset = mp_index % 2 * own_width
    keys_out = lax.dynamic_slice_in_dim(keys_rot, offset, own_width, 1)
    values_out = lax.dynamic_slice_in_dim(values_all, offset, own_width, 1)
    return (residual, hidden, keys_out, values_out)


def solution(mesh):
    in_specs = (
        P(("dp", "mp"), None),
        P("dp"),
        P(),
        P("dp", "mp"),
        P("dp", "mp"),
        P("dp", "mp"),
        P("mp", None),
        P(),
        P(),
        P("dp", "mp"),
        P("dp", "mp"),
    )
    out_specs = (P(("dp", "mp"), None), P("dp", "mp"), P("dp", "mp"), P("dp", "mp"))
    return jax.shard_map(
        on_device, mesh=mesh, in_specs=in_specs, out_specs=out_specs, check_vma=False
    )
```

```python
import math

import jax
import jax.numpy as jnp
from jax import lax
from jax.sharding import PartitionSpec as P

query_scale = 1.0 / 12.0
soft_cap = 50.0


def permute(value, axis, target):
    return lax.ppermute(value, axis, [(k, target(k)) for k in range(lax.axis_size(axis))])


def gather_dp_start(value):
    count = lax.axis_size("dp")
    partner = permute(value, "dp", lambda k: k ^ 1)
    if count != 8:
        return (partner,)
    from_below = permute(value, "dp", lambda k: (k + 2) % count)
    from_above = permute(value, "dp", lambda k: (k - 2) % count)
    return (partner, from_below, from_above)


def gather_dp_finish(value, started, tie=None):
    count = lax.axis_size("dp")
    index = lax.axis_index("dp")
    if count != 8:
        full = gather_dp_direct(value, started[0])
        return full if tie is None else (full, tie)
    partner, from_below, from_above = started
    half = value.shape[0] // 2
    up = lambda k: (k + 2) % count
    down = lambda k: (k - 2) % count
    partner_below = permute(partner, "dp", up)
    partner_above = permute(partner, "dp", down)
    far_low = permute(from_below[:half], "dp", up)
    far_high = permute(from_above[half:], "dp", down)
    if tie is not None:
        (partner_below, partner_above, far_low, far_high), tie = lax.optimization_barrier(
            ((partner_below, partner_above, far_low, far_high), tie)
        )
    far_partner_low = permute(partner_below[:half], "dp", up)
    far_partner_high = permute(partner_above[half:], "dp", down)
    pieces = [
        (value, index),
        (partner, index ^ 1),
        (from_below, (index - 2) % count),
        (from_above, (index + 2) % count),
        (partner_below, ((index - 2) % count) ^ 1),
        (partner_above, ((index + 2) % count) ^ 1),
        (jnp.concatenate([far_low, far_high]), (index + 4) % count),
        (jnp.concatenate([far_partner_low, far_partner_high]), ((index + 4) % count) ^ 1),
    ]
    stacked = jnp.zeros((count,) + value.shape, value.dtype)
    for piece, where in pieces:
        stacked = lax.dynamic_update_index_in_dim(stacked, piece, where, 0)
    full = stacked.reshape(count * value.shape[0], value.shape[1])
    return full if tie is None else (full, tie)


def gather_dp(value):
    return gather_dp_finish(value, gather_dp_start(value))


def gather_dp_direct(value, partner):
    count = lax.axis_size("dp")
    index = lax.axis_index("dp")
    pieces = [(value, index), (partner, index ^ 1)]
    for step in range(1, count // 2):
        got = permute(value, "dp", lambda k, step=step: (k + 2 * step) % count)
        pieces.append((got, (index - 2 * step) % count))
    for step in range(1, count // 2):
        got = permute(partner, "dp", lambda k, step=step: (k + 2 * step) % count)
        pieces.append((got, ((index - 2 * step) % count) ^ 1))
    stacked = jnp.zeros((count,) + value.shape, value.dtype)
    for piece, where in pieces:
        stacked = lax.dynamic_update_index_in_dim(stacked, piece, where, 0)
    return stacked.reshape(count * value.shape[0], value.shape[1])


def pair_order(value, other, low_flag, axis):
    lower = jnp.where(low_flag, value, other)
    upper = jnp.where(low_flag, other, value)
    return jnp.stack([lower, upper], axis=axis)


def chip_orders(chip_bits):
    if chip_bits == 4:
        return [1, 3, 0, 2], [3, 1, 2, 0]
    return list(range(chip_bits)), list(range(chip_bits))


def bit_by_core(index, even_bits, odd_bits, step):
    return jnp.where(index % 2 == 0, even_bits[step], odd_bits[step])


def step_partner(even_bit, odd_bit):
    return lambda k: k ^ (2 << (even_bit if k % 2 == 0 else odd_bit))


def to_bit_order(stacked, axis_bits, chip_bits):
    return stacked.transpose([axis_bits.index(b) for b in range(chip_bits - 1, -1, -1)] + list(range(chip_bits, stacked.ndim)))


def gather_mp(value):
    count = lax.axis_size("mp")
    index = lax.axis_index("mp")
    chip_bits = (count // 2).bit_length() - 1
    even_bits, odd_bits = chip_orders(chip_bits)
    stacked = value
    for step in range(chip_bits):
        other = permute(stacked, "mp", step_partner(even_bits[step], odd_bits[step]))
        bit = bit_by_core(index, even_bits, odd_bits, step)
        stacked = pair_order(stacked, other, (index >> (bit + 1)) % 2 == 0, 0)
    even_axes = list(reversed(even_bits))
    odd_axes = list(reversed(odd_bits))
    stacked = jnp.where(
        index % 2 == 0,
        to_bit_order(stacked, even_axes, chip_bits),
        to_bit_order(stacked, odd_axes, chip_bits),
    )
    other = permute(stacked, "mp", lambda k: k ^ 1)
    stacked = pair_order(stacked, other, index % 2 == 0, chip_bits)
    return stacked.reshape(count * value.shape[0], value.shape[1])


def from_bit_order(blocks, step_bits, chip_bits):
    return blocks.transpose([chip_bits - 1 - b for b in step_bits] + list(range(chip_bits, blocks.ndim)))


def reduce_scatter_mp(value):
    count = lax.axis_size("mp")
    index = lax.axis_index("mp")
    chip_bits = (count // 2).bit_length() - 1
    rows = value.shape[0] // count
    even_bits, odd_bits = chip_orders(chip_bits)
    even_bits, odd_bits = even_bits[::-1], odd_bits[::-1]
    blocks = value.reshape([2] * chip_bits + [2, rows, value.shape[1]])
    core = index % 2
    mine = lax.dynamic_index_in_dim(blocks, core, chip_bits, keepdims=False)
    theirs = lax.dynamic_index_in_dim(blocks, 1 - core, chip_bits, keepdims=False)
    got = permute(theirs, "mp", lambda k: k ^ 1)
    total = mine.astype(jnp.float32) + got.astype(jnp.float32)
    total = jnp.where(
        index % 2 == 0,
        from_bit_order(total, even_bits, chip_bits),
        from_bit_order(total, odd_bits, chip_bits),
    )
    for step in range(chip_bits):
        bit = bit_by_core(index, even_bits, odd_bits, step)
        mine_bit = (index >> (bit + 1)) % 2
        keep = lax.dynamic_index_in_dim(total, mine_bit, 0, keepdims=False)
        send = lax.dynamic_index_in_dim(total, 1 - mine_bit, 0, keepdims=False)
        got = permute(
            send.astype(jnp.bfloat16), "mp", step_partner(even_bits[step], odd_bits[step])
        )
        total = keep + got.astype(jnp.float32)
    return total


def rms_norm(values, gain):
    mean_sq = jnp.mean(values * values, axis=-1, keepdims=True)
    return values * lax.rsqrt(mean_sq + 1e-06) * gain


def rotate_pairs(values, positions):
    half_size = values.shape[-1] // 2
    freqs = jnp.exp(
        jnp.arange(half_size, dtype=jnp.float32) * (-2.0 * math.log(10000.0) / values.shape[-1])
    )
    angles = positions.astype(jnp.float32)[:, None] * freqs[None, :]
    cosine = jnp.cos(angles)[:, None, :]
    sine = jnp.sin(angles)[:, None, :]
    first = values[..., :half_size]
    second = values[..., half_size:]
    return jnp.concatenate(
        [first * cosine - second * sine, second * cosine + first * sine], axis=-1
    )


def join_halves(own_half, other_half, odd_flag):
    lower_first = jnp.concatenate([own_half, other_half], axis=1)
    upper_first = jnp.concatenate([other_half, own_half], axis=1)
    return jnp.where(odd_flag, upper_first, lower_first)


def head_block(query_rows, key_rows, value_rows, key_count, length):
    scores = (
        jnp.einsum("qhd,kd->hqk", query_rows, key_rows, preferred_element_type=jnp.float32)
        * query_scale
    )
    capped = soft_cap * jnp.tanh(scores / soft_cap)
    query_pos = jnp.arange(query_rows.shape[0], dtype=jnp.int32)
    key_pos = jnp.arange(key_count, dtype=jnp.int32)
    allowed = (key_pos[None, :] <= query_pos[:, None]) & (key_pos[None, :] < length)
    weights_exp = jnp.where(allowed[None], jnp.exp(capped), jnp.float32(0.0))
    probs = (weights_exp / jnp.sum(weights_exp, axis=-1, keepdims=True)).astype(jnp.bfloat16)
    return jnp.einsum("hqk,kd->qhd", probs, value_rows, preferred_element_type=jnp.float32)


def on_device(
    inputs,
    lengths,
    gain_in,
    query_weight,
    key_weight,
    value_weight,
    output_weight,
    gain_post,
    gain_pre,
    gate_weight,
    up_weight,
):
    mp_index = lax.axis_index("mp")
    odd_flag = mp_index % 2 == 1
    query_width = query_weight.shape[1]
    own_width = key_weight.shape[1]
    ffn_width = gate_weight.shape[1]
    qkv_own = jnp.concatenate(
        [query_weight, key_weight, value_weight], axis=1
    ).astype(jnp.bfloat16)
    ffn_own = jnp.concatenate([gate_weight, up_weight], axis=1).astype(jnp.bfloat16)
    qkv_full = gather_dp(qkv_own)
    ffn_started = gather_dp_start(ffn_own)

    normed_local = rms_norm(inputs.astype(jnp.float32), gain_in).astype(jnp.bfloat16)
    normed = gather_mp(normed_local)
    group_tokens = normed.shape[0]
    slot = group_tokens

    raw = jnp.dot(normed, qkv_full, preferred_element_type=jnp.float32)
    raw_q = raw[:, :query_width]
    raw_kv_own = raw[:, query_width:]
    raw_kv_other = permute(raw_kv_own, "mp", lambda k: k ^ 1)
    raw_k = join_halves(raw_kv_own[:, :own_width], raw_kv_other[:, :own_width], odd_flag)
    raw_v = join_halves(raw_kv_own[:, own_width:], raw_kv_other[:, own_width:], odd_flag)

    head_size = raw_k.shape[1]
    local_heads = raw_q.shape[1] // head_size
    positions = jnp.arange(group_tokens, dtype=jnp.int32)
    length = lengths[0]
    live = positions < length
    queries = rotate_pairs(raw_q.reshape(group_tokens, local_heads, head_size), positions).astype(
        jnp.bfloat16
    )
    keys_rot = rotate_pairs(raw_k.reshape(group_tokens, 1, head_size), positions).reshape(
        group_tokens, head_size
    )
    keys_rot = jnp.where(live[:, None], keys_rot, jnp.float32(0.0)).astype(jnp.bfloat16)
    values_all = jnp.where(live[:, None], raw_v, jnp.float32(0.0)).astype(jnp.bfloat16)
    mixed = head_block(queries, keys_rot, values_all, slot, length)
    mixed = jnp.where(live[:, None, None], mixed, jnp.float32(0.0))
    attended = mixed.astype(jnp.bfloat16).reshape(slot, local_heads * head_size)
    partial = jnp.dot(attended, output_weight, preferred_element_type=jnp.float32).astype(
        jnp.bfloat16
    )
    ffn_started, partial = lax.optimization_barrier((ffn_started, partial))
    attn_rows = reduce_scatter_mp(partial)
    residual = (inputs.astype(jnp.float32) + rms_norm(attn_rows, gain_post)).astype(jnp.bfloat16)
    pre_local = rms_norm(residual.astype(jnp.float32), gain_pre).astype(jnp.bfloat16)
    ffn_full = gather_dp_finish(ffn_own, ffn_started)
    pre_ffn = gather_mp(pre_local)
    ffn_full, pre_ffn = lax.optimization_barrier((ffn_full, pre_ffn))
    both = jnp.dot(pre_ffn, ffn_full, preferred_element_type=jnp.float32)
    gate = both[:, :ffn_width]
    up_part = both[:, ffn_width:]
    hidden = (jax.nn.gelu(gate, approximate=True) * up_part).astype(jnp.bfloat16)
    offset = mp_index % 2 * own_width
    keys_out = lax.dynamic_slice_in_dim(keys_rot, offset, own_width, 1)
    values_out = lax.dynamic_slice_in_dim(values_all, offset, own_width, 1)
    return (residual, hidden, keys_out, values_out)


def solution(mesh):
    in_specs = (
        P(("dp", "mp"), None),
        P("dp"),
        P(),
        P("dp", "mp"),
        P("dp", "mp"),
        P("dp", "mp"),
        P("mp", None),
        P(),
        P(),
        P("dp", "mp"),
        P("dp", "mp"),
    )
    out_specs = (P(("dp", "mp"), None), P("dp", "mp"), P("dp", "mp"), P("dp", "mp"))
    return jax.shard_map(
        on_device, mesh=mesh, in_specs=in_specs, out_specs=out_specs, check_vma=False
    )
```

```python
import math

import jax
import jax.numpy as jnp
from jax import lax
from jax.sharding import PartitionSpec as P

query_scale = 1.0 / 12.0
soft_cap = 50.0


def permute(value, axis, target):
    return lax.ppermute(value, axis, [(k, target(k)) for k in range(lax.axis_size(axis))])


def gather_dp_start(value):
    count = lax.axis_size("dp")
    partner = permute(value, "dp", lambda k: k ^ 1)
    if count != 8:
        return (partner,)
    from_below = permute(value, "dp", lambda k: (k + 2) % count)
    from_above = permute(value, "dp", lambda k: (k - 2) % count)
    return (partner, from_below, from_above)


def gather_dp_relay(value, started):
    count = lax.axis_size("dp")
    partner, from_below, from_above = started
    half = value.shape[0] // 2
    up = lambda k: (k + 2) % count
    down = lambda k: (k - 2) % count
    return (
        permute(partner, "dp", up),
        permute(partner, "dp", down),
        permute(from_below[:half], "dp", up),
        permute(from_above[half:], "dp", down),
    )


def gather_dp_finish(value, started, relayed=None):
    count = lax.axis_size("dp")
    index = lax.axis_index("dp")
    if count != 8:
        return gather_dp_direct(value, started[0])
    if relayed is None:
        relayed = gather_dp_relay(value, started)
    partner, from_below, from_above = started
    partner_below, partner_above, far_low, far_high = relayed
    half = value.shape[0] // 2
    far_partner_low = permute(partner_below[:half], "dp", lambda k: (k + 2) % count)
    far_partner_high = permute(partner_above[half:], "dp", lambda k: (k - 2) % count)
    pieces = [
        (value, index),
        (partner, index ^ 1),
        (from_below, (index - 2) % count),
        (from_above, (index + 2) % count),
        (partner_below, ((index - 2) % count) ^ 1),
        (partner_above, ((index + 2) % count) ^ 1),
        (jnp.concatenate([far_low, far_high]), (index + 4) % count),
        (jnp.concatenate([far_partner_low, far_partner_high]), ((index + 4) % count) ^ 1),
    ]
    stacked = jnp.zeros((count,) + value.shape, value.dtype)
    for piece, where in pieces:
        stacked = lax.dynamic_update_index_in_dim(stacked, piece, where, 0)
    return stacked.reshape(count * value.shape[0], value.shape[1])


def gather_dp(value):
    return gather_dp_finish(value, gather_dp_start(value))


def gather_dp_direct(value, partner):
    count = lax.axis_size("dp")
    index = lax.axis_index("dp")
    pieces = [(value, index), (partner, index ^ 1)]
    for step in range(1, count // 2):
        got = permute(value, "dp", lambda k, step=step: (k + 2 * step) % count)
        pieces.append((got, (index - 2 * step) % count))
    for step in range(1, count // 2):
        got = permute(partner, "dp", lambda k, step=step: (k + 2 * step) % count)
        pieces.append((got, ((index - 2 * step) % count) ^ 1))
    stacked = jnp.zeros((count,) + value.shape, value.dtype)
    for piece, where in pieces:
        stacked = lax.dynamic_update_index_in_dim(stacked, piece, where, 0)
    return stacked.reshape(count * value.shape[0], value.shape[1])


def pair_order(value, other, low_flag, axis):
    lower = jnp.where(low_flag, value, other)
    upper = jnp.where(low_flag, other, value)
    return jnp.stack([lower, upper], axis=axis)


def chip_orders(chip_bits):
    if chip_bits == 4:
        return [1, 3, 0, 2], [3, 1, 2, 0]
    return list(range(chip_bits)), list(range(chip_bits))


def bit_by_core(index, even_bits, odd_bits, step):
    return jnp.where(index % 2 == 0, even_bits[step], odd_bits[step])


def step_partner(even_bit, odd_bit):
    return lambda k: k ^ (2 << (even_bit if k % 2 == 0 else odd_bit))


def to_bit_order(stacked, axis_bits, chip_bits):
    return stacked.transpose([axis_bits.index(b) for b in range(chip_bits - 1, -1, -1)] + list(range(chip_bits, stacked.ndim)))


def gather_mp(value, tie=None, tie_step=0):
    count = lax.axis_size("mp")
    index = lax.axis_index("mp")
    chip_bits = (count // 2).bit_length() - 1
    even_bits, odd_bits = chip_orders(chip_bits)
    stacked = value
    for step in range(chip_bits):
        if tie is not None and step == min(tie_step, chip_bits - 1):
            stacked, tie = lax.optimization_barrier((stacked, tie))
        other = permute(stacked, "mp", step_partner(even_bits[step], odd_bits[step]))
        bit = bit_by_core(index, even_bits, odd_bits, step)
        stacked = pair_order(stacked, other, (index >> (bit + 1)) % 2 == 0, 0)
    even_axes = list(reversed(even_bits))
    odd_axes = list(reversed(odd_bits))
    stacked = jnp.where(
        index % 2 == 0,
        to_bit_order(stacked, even_axes, chip_bits),
        to_bit_order(stacked, odd_axes, chip_bits),
    )
    other = permute(stacked, "mp", lambda k: k ^ 1)
    stacked = pair_order(stacked, other, index % 2 == 0, chip_bits)
    full = stacked.reshape(count * value.shape[0], value.shape[1])
    return full if tie is None else (full, tie)


def from_bit_order(blocks, step_bits, chip_bits):
    return blocks.transpose([chip_bits - 1 - b for b in step_bits] + list(range(chip_bits, blocks.ndim)))


def reduce_scatter_mp(value):
    count = lax.axis_size("mp")
    index = lax.axis_index("mp")
    chip_bits = (count // 2).bit_length() - 1
    rows = value.shape[0] // count
    even_bits, odd_bits = chip_orders(chip_bits)
    even_bits, odd_bits = even_bits[::-1], odd_bits[::-1]
    blocks = value.reshape([2] * chip_bits + [2, rows, value.shape[1]])
    core = index % 2
    mine = lax.dynamic_index_in_dim(blocks, core, chip_bits, keepdims=False)
    theirs = lax.dynamic_index_in_dim(blocks, 1 - core, chip_bits, keepdims=False)
    got = permute(theirs, "mp", lambda k: k ^ 1)
    total = mine.astype(jnp.float32) + got.astype(jnp.float32)
    total = jnp.where(
        index % 2 == 0,
        from_bit_order(total, even_bits, chip_bits),
        from_bit_order(total, odd_bits, chip_bits),
    )
    for step in range(chip_bits):
        bit = bit_by_core(index, even_bits, odd_bits, step)
        mine_bit = (index >> (bit + 1)) % 2
        keep = lax.dynamic_index_in_dim(total, mine_bit, 0, keepdims=False)
        send = lax.dynamic_index_in_dim(total, 1 - mine_bit, 0, keepdims=False)
        got = permute(
            send.astype(jnp.bfloat16), "mp", step_partner(even_bits[step], odd_bits[step])
        )
        total = keep + got.astype(jnp.float32)
    return total


def rms_norm(values, gain):
    mean_sq = jnp.mean(values * values, axis=-1, keepdims=True)
    return values * lax.rsqrt(mean_sq + 1e-06) * gain


def rotate_pairs(values, positions):
    half_size = values.shape[-1] // 2
    freqs = jnp.exp(
        jnp.arange(half_size, dtype=jnp.float32) * (-2.0 * math.log(10000.0) / values.shape[-1])
    )
    angles = positions.astype(jnp.float32)[:, None] * freqs[None, :]
    cosine = jnp.cos(angles)[:, None, :]
    sine = jnp.sin(angles)[:, None, :]
    first = values[..., :half_size]
    second = values[..., half_size:]
    return jnp.concatenate(
        [first * cosine - second * sine, second * cosine + first * sine], axis=-1
    )


def join_halves(own_half, other_half, odd_flag):
    lower_first = jnp.concatenate([own_half, other_half], axis=1)
    upper_first = jnp.concatenate([other_half, own_half], axis=1)
    return jnp.where(odd_flag, upper_first, lower_first)


def head_block(query_rows, key_rows, value_rows, key_count, length):
    scores = (
        jnp.einsum("qhd,kd->hqk", query_rows, key_rows, preferred_element_type=jnp.float32)
        * query_scale
    )
    capped = soft_cap * jnp.tanh(scores / soft_cap)
    query_pos = jnp.arange(query_rows.shape[0], dtype=jnp.int32)
    key_pos = jnp.arange(key_count, dtype=jnp.int32)
    allowed = (key_pos[None, :] <= query_pos[:, None]) & (key_pos[None, :] < length)
    weights_exp = jnp.where(allowed[None], jnp.exp(capped), jnp.float32(0.0))
    probs = (weights_exp / jnp.sum(weights_exp, axis=-1, keepdims=True)).astype(jnp.bfloat16)
    return jnp.einsum("hqk,kd->qhd", probs, value_rows, preferred_element_type=jnp.float32)


def on_device(
    inputs,
    lengths,
    gain_in,
    query_weight,
    key_weight,
    value_weight,
    output_weight,
    gain_post,
    gain_pre,
    gate_weight,
    up_weight,
):
    mp_index = lax.axis_index("mp")
    odd_flag = mp_index % 2 == 1
    query_width = query_weight.shape[1]
    own_width = key_weight.shape[1]
    ffn_width = gate_weight.shape[1]
    qkv_own = jnp.concatenate(
        [query_weight, key_weight, value_weight], axis=1
    ).astype(jnp.bfloat16)
    ffn_own = jnp.concatenate([gate_weight, up_weight], axis=1).astype(jnp.bfloat16)
    qkv_full = gather_dp(qkv_own)
    ffn_started = gather_dp_start(ffn_own)

    normed_local = rms_norm(inputs.astype(jnp.float32), gain_in).astype(jnp.bfloat16)
    normed = gather_mp(normed_local)
    group_tokens = normed.shape[0]
    slot = group_tokens

    raw = jnp.dot(normed, qkv_full, preferred_element_type=jnp.float32)
    raw_q = raw[:, :query_width]
    raw_kv_own = raw[:, query_width:]
    raw_kv_other = permute(raw_kv_own, "mp", lambda k: k ^ 1)
    raw_k = join_halves(raw_kv_own[:, :own_width], raw_kv_other[:, :own_width], odd_flag)
    raw_v = join_halves(raw_kv_own[:, own_width:], raw_kv_other[:, own_width:], odd_flag)

    head_size = raw_k.shape[1]
    local_heads = raw_q.shape[1] // head_size
    positions = jnp.arange(group_tokens, dtype=jnp.int32)
    length = lengths[0]
    live = positions < length
    queries = rotate_pairs(raw_q.reshape(group_tokens, local_heads, head_size), positions).astype(
        jnp.bfloat16
    )
    keys_rot = rotate_pairs(raw_k.reshape(group_tokens, 1, head_size), positions).reshape(
        group_tokens, head_size
    )
    keys_rot = jnp.where(live[:, None], keys_rot, jnp.float32(0.0)).astype(jnp.bfloat16)
    values_all = jnp.where(live[:, None], raw_v, jnp.float32(0.0)).astype(jnp.bfloat16)
    mixed = head_block(queries, keys_rot, values_all, slot, length)
    mixed = jnp.where(live[:, None, None], mixed, jnp.float32(0.0))
    attended = mixed.astype(jnp.bfloat16).reshape(slot, local_heads * head_size)
    partial = jnp.dot(attended, output_weight, preferred_element_type=jnp.float32).astype(
        jnp.bfloat16
    )
    ffn_started, partial = lax.optimization_barrier((ffn_started, partial))
    attn_rows = reduce_scatter_mp(partial)
    residual = (inputs.astype(jnp.float32) + rms_norm(attn_rows, gain_post)).astype(jnp.bfloat16)
    pre_local = rms_norm(residual.astype(jnp.float32), gain_pre).astype(jnp.bfloat16)
    if lax.axis_size("dp") == 8:
        relayed = gather_dp_relay(ffn_own, ffn_started)
        pre_ffn, relayed = gather_mp(pre_local, relayed, 3)
    else:
        pre_ffn, relayed = gather_mp(pre_local), None
    ffn_full = gather_dp_finish(ffn_own, ffn_started, relayed)
    ffn_full, pre_ffn = lax.optimization_barrier((ffn_full, pre_ffn))
    both = jnp.dot(pre_ffn, ffn_full, preferred_element_type=jnp.float32)
    gate = both[:, :ffn_width]
    up_part = both[:, ffn_width:]
    hidden = (jax.nn.gelu(gate, approximate=True) * up_part).astype(jnp.bfloat16)
    offset = mp_index % 2 * own_width
    keys_out = lax.dynamic_slice_in_dim(keys_rot, offset, own_width, 1)
    values_out = lax.dynamic_slice_in_dim(values_all, offset, own_width, 1)
    return (residual, hidden, keys_out, values_out)


def solution(mesh):
    in_specs = (
        P(("dp", "mp"), None),
        P("dp"),
        P(),
        P("dp", "mp"),
        P("dp", "mp"),
        P("dp", "mp"),
        P("mp", None),
        P(),
        P(),
        P("dp", "mp"),
        P("dp", "mp"),
    )
    out_specs = (P(("dp", "mp"), None), P("dp", "mp"), P("dp", "mp"), P("dp", "mp"))
    return jax.shard_map(
        on_device, mesh=mesh, in_specs=in_specs, out_specs=out_specs, check_vma=False
    )
```

```python
import math

import jax
import jax.numpy as jnp
from jax import lax
from jax.sharding import PartitionSpec as P

query_scale = 1.0 / 12.0
soft_cap = 50.0


def permute(value, axis, target):
    return lax.ppermute(value, axis, [(k, target(k)) for k in range(lax.axis_size(axis))])


def gather_dp_start(value):
    count = lax.axis_size("dp")
    partner = permute(value, "dp", lambda k: k ^ 1)
    if count != 8:
        return (partner,)
    from_below = permute(value, "dp", lambda k: (k + 2) % count)
    from_above = permute(value, "dp", lambda k: (k - 2) % count)
    return (partner, from_below, from_above)


def gather_dp_relay(value, started):
    count = lax.axis_size("dp")
    partner, from_below, from_above = started
    half = value.shape[0] // 2
    up = lambda k: (k + 2) % count
    down = lambda k: (k - 2) % count
    return (
        permute(partner, "dp", up),
        permute(partner, "dp", down),
        permute(from_below[:half], "dp", up),
        permute(from_above[half:], "dp", down),
    )


def gather_dp_finish(value, started, relayed=None):
    count = lax.axis_size("dp")
    index = lax.axis_index("dp")
    if count != 8:
        return gather_dp_direct(value, started[0])
    if relayed is None:
        relayed = gather_dp_relay(value, started)
    partner, from_below, from_above = started
    partner_below, partner_above, far_low, far_high = relayed
    half = value.shape[0] // 2
    far_partner_low = permute(partner_below[:half], "dp", lambda k: (k + 2) % count)
    far_partner_high = permute(partner_above[half:], "dp", lambda k: (k - 2) % count)
    pieces = [
        (value, index),
        (partner, index ^ 1),
        (from_below, (index - 2) % count),
        (from_above, (index + 2) % count),
        (partner_below, ((index - 2) % count) ^ 1),
        (partner_above, ((index + 2) % count) ^ 1),
        (jnp.concatenate([far_low, far_high]), (index + 4) % count),
        (jnp.concatenate([far_partner_low, far_partner_high]), ((index + 4) % count) ^ 1),
    ]
    stacked = jnp.zeros((count,) + value.shape, value.dtype)
    for piece, where in pieces:
        stacked = lax.dynamic_update_index_in_dim(stacked, piece, where, 0)
    return stacked.reshape(count * value.shape[0], value.shape[1])


def gather_dp(value):
    return gather_dp_finish(value, gather_dp_start(value))


def gather_dp_direct(value, partner):
    count = lax.axis_size("dp")
    index = lax.axis_index("dp")
    pieces = [(value, index), (partner, index ^ 1)]
    for step in range(1, count // 2):
        got = permute(value, "dp", lambda k, step=step: (k + 2 * step) % count)
        pieces.append((got, (index - 2 * step) % count))
    for step in range(1, count // 2):
        got = permute(partner, "dp", lambda k, step=step: (k + 2 * step) % count)
        pieces.append((got, ((index - 2 * step) % count) ^ 1))
    stacked = jnp.zeros((count,) + value.shape, value.dtype)
    for piece, where in pieces:
        stacked = lax.dynamic_update_index_in_dim(stacked, piece, where, 0)
    return stacked.reshape(count * value.shape[0], value.shape[1])


def pair_order(value, other, low_flag, axis):
    lower = jnp.where(low_flag, value, other)
    upper = jnp.where(low_flag, other, value)
    return jnp.stack([lower, upper], axis=axis)


def chip_orders(chip_bits):
    if chip_bits == 4:
        return [1, 3, 0, 2], [3, 1, 2, 0]
    return list(range(chip_bits)), list(range(chip_bits))


def bit_by_core(index, even_bits, odd_bits, step):
    return jnp.where(index % 2 == 0, even_bits[step], odd_bits[step])


def step_partner(even_bit, odd_bit):
    return lambda k: k ^ (2 << (even_bit if k % 2 == 0 else odd_bit))


def to_bit_order(stacked, axis_bits, chip_bits):
    return stacked.transpose([axis_bits.index(b) for b in range(chip_bits - 1, -1, -1)] + list(range(chip_bits, stacked.ndim)))


def gather_mp(value, tie=None, tie_step=0):
    count = lax.axis_size("mp")
    index = lax.axis_index("mp")
    chip_bits = (count // 2).bit_length() - 1
    even_bits, odd_bits = chip_orders(chip_bits)
    stacked = value
    for step in range(chip_bits):
        if tie is not None and step == min(tie_step, chip_bits - 1):
            stacked, tie = lax.optimization_barrier((stacked, tie))
        other = permute(stacked, "mp", step_partner(even_bits[step], odd_bits[step]))
        bit = bit_by_core(index, even_bits, odd_bits, step)
        stacked = pair_order(stacked, other, (index >> (bit + 1)) % 2 == 0, 0)
    even_axes = list(reversed(even_bits))
    odd_axes = list(reversed(odd_bits))
    stacked = jnp.where(
        index % 2 == 0,
        to_bit_order(stacked, even_axes, chip_bits),
        to_bit_order(stacked, odd_axes, chip_bits),
    )
    other = permute(stacked, "mp", lambda k: k ^ 1)
    stacked = pair_order(stacked, other, index % 2 == 0, chip_bits)
    full = stacked.reshape(count * value.shape[0], value.shape[1])
    return full if tie is None else (full, tie)


def from_bit_order(blocks, step_bits, chip_bits):
    return blocks.transpose([chip_bits - 1 - b for b in step_bits] + list(range(chip_bits, blocks.ndim)))


def reduce_scatter_mp(value):
    count = lax.axis_size("mp")
    index = lax.axis_index("mp")
    chip_bits = (count // 2).bit_length() - 1
    rows = value.shape[0] // count
    even_bits, odd_bits = chip_orders(chip_bits)
    even_bits, odd_bits = even_bits[::-1], odd_bits[::-1]
    blocks = value.reshape([2] * chip_bits + [2, rows, value.shape[1]])
    core = index % 2
    mine = lax.dynamic_index_in_dim(blocks, core, chip_bits, keepdims=False)
    theirs = lax.dynamic_index_in_dim(blocks, 1 - core, chip_bits, keepdims=False)
    got = permute(theirs, "mp", lambda k: k ^ 1)
    total = mine.astype(jnp.float32) + got.astype(jnp.float32)
    total = jnp.where(
        index % 2 == 0,
        from_bit_order(total, even_bits, chip_bits),
        from_bit_order(total, odd_bits, chip_bits),
    )
    for step in range(chip_bits):
        bit = bit_by_core(index, even_bits, odd_bits, step)
        mine_bit = (index >> (bit + 1)) % 2
        keep = lax.dynamic_index_in_dim(total, mine_bit, 0, keepdims=False)
        send = lax.dynamic_index_in_dim(total, 1 - mine_bit, 0, keepdims=False)
        got = permute(
            send.astype(jnp.bfloat16), "mp", step_partner(even_bits[step], odd_bits[step])
        )
        total = keep + got.astype(jnp.float32)
    return total


def rms_norm(values, gain):
    mean_sq = jnp.mean(values * values, axis=-1, keepdims=True)
    return values * lax.rsqrt(mean_sq + 1e-06) * gain


def rotate_pairs(values, positions):
    half_size = values.shape[-1] // 2
    freqs = jnp.exp(
        jnp.arange(half_size, dtype=jnp.float32) * (-2.0 * math.log(10000.0) / values.shape[-1])
    )
    angles = positions.astype(jnp.float32)[:, None] * freqs[None, :]
    cosine = jnp.cos(angles)[:, None, :]
    sine = jnp.sin(angles)[:, None, :]
    first = values[..., :half_size]
    second = values[..., half_size:]
    return jnp.concatenate(
        [first * cosine - second * sine, second * cosine + first * sine], axis=-1
    )


def join_halves(own_half, other_half, odd_flag):
    lower_first = jnp.concatenate([own_half, other_half], axis=1)
    upper_first = jnp.concatenate([other_half, own_half], axis=1)
    return jnp.where(odd_flag, upper_first, lower_first)


def head_block(query_rows, key_rows, value_rows, key_count, length):
    scores = (
        jnp.einsum("qhd,kd->hqk", query_rows, key_rows, preferred_element_type=jnp.float32)
        * query_scale
    )
    capped = soft_cap * jnp.tanh(scores / soft_cap)
    query_pos = jnp.arange(query_rows.shape[0], dtype=jnp.int32)
    key_pos = jnp.arange(key_count, dtype=jnp.int32)
    allowed = (key_pos[None, :] <= query_pos[:, None]) & (key_pos[None, :] < length)
    weights_exp = jnp.where(allowed[None], jnp.exp(capped), jnp.float32(0.0))
    probs = (weights_exp / jnp.sum(weights_exp, axis=-1, keepdims=True)).astype(jnp.bfloat16)
    return jnp.einsum("hqk,kd->qhd", probs, value_rows, preferred_element_type=jnp.float32)


def on_device(
    inputs,
    lengths,
    gain_in,
    query_weight,
    key_weight,
    value_weight,
    output_weight,
    gain_post,
    gain_pre,
    gate_weight,
    up_weight,
):
    mp_index = lax.axis_index("mp")
    odd_flag = mp_index % 2 == 1
    query_width = query_weight.shape[1]
    own_width = key_weight.shape[1]
    ffn_width = gate_weight.shape[1]
    qkv_own = jnp.concatenate(
        [query_weight, key_weight, value_weight], axis=1
    ).astype(jnp.bfloat16)
    ffn_own = jnp.concatenate([gate_weight, up_weight], axis=1).astype(jnp.bfloat16)
    qkv_full = gather_dp(qkv_own)
    ffn_started = gather_dp_start(ffn_own)

    normed_local = rms_norm(inputs.astype(jnp.float32), gain_in).astype(jnp.bfloat16)
    normed = gather_mp(normed_local)
    ffn_started, normed = lax.optimization_barrier((ffn_started, normed))
    relay = lax.axis_size("dp") == 8
    relayed = gather_dp_relay(ffn_own, ffn_started) if relay else None
    group_tokens = normed.shape[0]
    slot = group_tokens

    raw = jnp.dot(normed, qkv_full, preferred_element_type=jnp.float32)
    raw_q = raw[:, :query_width]
    raw_kv_own = raw[:, query_width:]
    raw_kv_other = permute(raw_kv_own, "mp", lambda k: k ^ 1)
    raw_k = join_halves(raw_kv_own[:, :own_width], raw_kv_other[:, :own_width], odd_flag)
    raw_v = join_halves(raw_kv_own[:, own_width:], raw_kv_other[:, own_width:], odd_flag)

    head_size = raw_k.shape[1]
    local_heads = raw_q.shape[1] // head_size
    positions = jnp.arange(group_tokens, dtype=jnp.int32)
    length = lengths[0]
    live = positions < length
    queries = rotate_pairs(raw_q.reshape(group_tokens, local_heads, head_size), positions).astype(
        jnp.bfloat16
    )
    keys_rot = rotate_pairs(raw_k.reshape(group_tokens, 1, head_size), positions).reshape(
        group_tokens, head_size
    )
    keys_rot = jnp.where(live[:, None], keys_rot, jnp.float32(0.0)).astype(jnp.bfloat16)
    values_all = jnp.where(live[:, None], raw_v, jnp.float32(0.0)).astype(jnp.bfloat16)
    mixed = head_block(queries, keys_rot, values_all, slot, length)
    mixed = jnp.where(live[:, None, None], mixed, jnp.float32(0.0))
    attended = mixed.astype(jnp.bfloat16).reshape(slot, local_heads * head_size)
    partial = jnp.dot(attended, output_weight, preferred_element_type=jnp.float32).astype(
        jnp.bfloat16
    )
    if relay:
        relayed, partial = lax.optimization_barrier((relayed, partial))
    ffn_full = gather_dp_finish(ffn_own, ffn_started, relayed)
    attn_rows = reduce_scatter_mp(partial)
    ffn_full, attn_rows = lax.optimization_barrier((ffn_full, attn_rows))
    residual = (inputs.astype(jnp.float32) + rms_norm(attn_rows, gain_post)).astype(jnp.bfloat16)
    pre_local = rms_norm(residual.astype(jnp.float32), gain_pre).astype(jnp.bfloat16)
    pre_ffn = gather_mp(pre_local)
    both = jnp.dot(pre_ffn, ffn_full, preferred_element_type=jnp.float32)
    gate = both[:, :ffn_width]
    up_part = both[:, ffn_width:]
    hidden = (jax.nn.gelu(gate, approximate=True) * up_part).astype(jnp.bfloat16)
    offset = mp_index % 2 * own_width
    keys_out = lax.dynamic_slice_in_dim(keys_rot, offset, own_width, 1)
    values_out = lax.dynamic_slice_in_dim(values_all, offset, own_width, 1)
    return (residual, hidden, keys_out, values_out)


def solution(mesh):
    in_specs = (
        P(("dp", "mp"), None),
        P("dp"),
        P(),
        P("dp", "mp"),
        P("dp", "mp"),
        P("dp", "mp"),
        P("mp", None),
        P(),
        P(),
        P("dp", "mp"),
        P("dp", "mp"),
    )
    out_specs = (P(("dp", "mp"), None), P("dp", "mp"), P("dp", "mp"), P("dp", "mp"))
    return jax.shard_map(
        on_device, mesh=mesh, in_specs=in_specs, out_specs=out_specs, check_vma=False
    )
```

```python
import math

import jax
import jax.numpy as jnp
from jax import lax
from jax.sharding import PartitionSpec as P

query_scale = 1.0 / 12.0
soft_cap = 50.0


def permute(value, axis, target):
    return lax.ppermute(value, axis, [(k, target(k)) for k in range(lax.axis_size(axis))])


def gather_dp_start(value):
    count = lax.axis_size("dp")
    partner = permute(value, "dp", lambda k: k ^ 1)
    if count != 8:
        return (partner,)
    up = lambda k: (k + 2) % count
    down = lambda k: (k - 2) % count
    return (
        partner,
        permute(value, "dp", up),
        permute(value, "dp", down),
        permute(partner, "dp", up),
        permute(partner, "dp", down),
    )


def gather_dp_finish(value, started, tie=None):
    count = lax.axis_size("dp")
    index = lax.axis_index("dp")
    if count != 8:
        full = gather_dp_direct(value, started[0])
        return full if tie is None else (full, tie)
    partner, from_below, from_above, partner_below, partner_above = started
    half = value.shape[0] // 2
    up = lambda k: (k + 2) % count
    down = lambda k: (k - 2) % count
    far_low = permute(from_below[:half], "dp", up)
    far_high = permute(from_above[half:], "dp", down)
    if tie is not None:
        (partner_below, partner_above, far_low, far_high), tie = lax.optimization_barrier(
            ((partner_below, partner_above, far_low, far_high), tie)
        )
    far_partner_low = permute(partner_below[:half], "dp", up)
    far_partner_high = permute(partner_above[half:], "dp", down)
    pieces = [
        (value, index),
        (partner, index ^ 1),
        (from_below, (index - 2) % count),
        (from_above, (index + 2) % count),
        (partner_below, ((index - 2) % count) ^ 1),
        (partner_above, ((index + 2) % count) ^ 1),
        (jnp.concatenate([far_low, far_high]), (index + 4) % count),
        (jnp.concatenate([far_partner_low, far_partner_high]), ((index + 4) % count) ^ 1),
    ]
    stacked = jnp.zeros((count,) + value.shape, value.dtype)
    for piece, where in pieces:
        stacked = lax.dynamic_update_index_in_dim(stacked, piece, where, 0)
    full = stacked.reshape(count * value.shape[0], value.shape[1])
    return full if tie is None else (full, tie)


def gather_dp(value):
    return gather_dp_finish(value, gather_dp_start(value))


def gather_dp_direct(value, partner):
    count = lax.axis_size("dp")
    index = lax.axis_index("dp")
    pieces = [(value, index), (partner, index ^ 1)]
    for step in range(1, count // 2):
        got = permute(value, "dp", lambda k, step=step: (k + 2 * step) % count)
        pieces.append((got, (index - 2 * step) % count))
    for step in range(1, count // 2):
        got = permute(partner, "dp", lambda k, step=step: (k + 2 * step) % count)
        pieces.append((got, ((index - 2 * step) % count) ^ 1))
    stacked = jnp.zeros((count,) + value.shape, value.dtype)
    for piece, where in pieces:
        stacked = lax.dynamic_update_index_in_dim(stacked, piece, where, 0)
    return stacked.reshape(count * value.shape[0], value.shape[1])


def pair_order(value, other, low_flag, axis):
    lower = jnp.where(low_flag, value, other)
    upper = jnp.where(low_flag, other, value)
    return jnp.stack([lower, upper], axis=axis)


def chip_orders(chip_bits):
    if chip_bits == 4:
        return [1, 3, 0, 2], [3, 1, 2, 0]
    return list(range(chip_bits)), list(range(chip_bits))


def bit_by_core(index, even_bits, odd_bits, step):
    return jnp.where(index % 2 == 0, even_bits[step], odd_bits[step])


def step_partner(even_bit, odd_bit):
    return lambda k: k ^ (2 << (even_bit if k % 2 == 0 else odd_bit))


def to_bit_order(stacked, axis_bits, chip_bits):
    return stacked.transpose([axis_bits.index(b) for b in range(chip_bits - 1, -1, -1)] + list(range(chip_bits, stacked.ndim)))


def gather_mp(value):
    count = lax.axis_size("mp")
    index = lax.axis_index("mp")
    chip_bits = (count // 2).bit_length() - 1
    even_bits, odd_bits = chip_orders(chip_bits)
    stacked = value
    for step in range(chip_bits):
        other = permute(stacked, "mp", step_partner(even_bits[step], odd_bits[step]))
        bit = bit_by_core(index, even_bits, odd_bits, step)
        stacked = pair_order(stacked, other, (index >> (bit + 1)) % 2 == 0, 0)
    even_axes = list(reversed(even_bits))
    odd_axes = list(reversed(odd_bits))
    stacked = jnp.where(
        index % 2 == 0,
        to_bit_order(stacked, even_axes, chip_bits),
        to_bit_order(stacked, odd_axes, chip_bits),
    )
    other = permute(stacked, "mp", lambda k: k ^ 1)
    stacked = pair_order(stacked, other, index % 2 == 0, chip_bits)
    return stacked.reshape(count * value.shape[0], value.shape[1])


def from_bit_order(blocks, step_bits, chip_bits):
    return blocks.transpose([chip_bits - 1 - b for b in step_bits] + list(range(chip_bits, blocks.ndim)))


def reduce_scatter_mp(value):
    count = lax.axis_size("mp")
    index = lax.axis_index("mp")
    chip_bits = (count // 2).bit_length() - 1
    rows = value.shape[0] // count
    even_bits, odd_bits = chip_orders(chip_bits)
    even_bits, odd_bits = even_bits[::-1], odd_bits[::-1]
    blocks = value.reshape([2] * chip_bits + [2, rows, value.shape[1]])
    core = index % 2
    mine = lax.dynamic_index_in_dim(blocks, core, chip_bits, keepdims=False)
    theirs = lax.dynamic_index_in_dim(blocks, 1 - core, chip_bits, keepdims=False)
    got = permute(theirs, "mp", lambda k: k ^ 1)
    total = mine.astype(jnp.float32) + got.astype(jnp.float32)
    total = jnp.where(
        index % 2 == 0,
        from_bit_order(total, even_bits, chip_bits),
        from_bit_order(total, odd_bits, chip_bits),
    )
    for step in range(chip_bits):
        bit = bit_by_core(index, even_bits, odd_bits, step)
        mine_bit = (index >> (bit + 1)) % 2
        keep = lax.dynamic_index_in_dim(total, mine_bit, 0, keepdims=False)
        send = lax.dynamic_index_in_dim(total, 1 - mine_bit, 0, keepdims=False)
        got = permute(
            send.astype(jnp.bfloat16), "mp", step_partner(even_bits[step], odd_bits[step])
        )
        total = keep + got.astype(jnp.float32)
    return total


def rms_norm(values, gain):
    mean_sq = jnp.mean(values * values, axis=-1, keepdims=True)
    return values * lax.rsqrt(mean_sq + 1e-06) * gain


def rotate_pairs(values, positions):
    half_size = values.shape[-1] // 2
    freqs = jnp.exp(
        jnp.arange(half_size, dtype=jnp.float32) * (-2.0 * math.log(10000.0) / values.shape[-1])
    )
    angles = positions.astype(jnp.float32)[:, None] * freqs[None, :]
    cosine = jnp.cos(angles)[:, None, :]
    sine = jnp.sin(angles)[:, None, :]
    first = values[..., :half_size]
    second = values[..., half_size:]
    return jnp.concatenate(
        [first * cosine - second * sine, second * cosine + first * sine], axis=-1
    )


def join_halves(own_half, other_half, odd_flag):
    lower_first = jnp.concatenate([own_half, other_half], axis=1)
    upper_first = jnp.concatenate([other_half, own_half], axis=1)
    return jnp.where(odd_flag, upper_first, lower_first)


def head_block(query_rows, key_rows, value_rows, key_count, length):
    scores = (
        jnp.einsum("qhd,kd->hqk", query_rows, key_rows, preferred_element_type=jnp.float32)
        * query_scale
    )
    capped = soft_cap * jnp.tanh(scores / soft_cap)
    query_pos = jnp.arange(query_rows.shape[0], dtype=jnp.int32)
    key_pos = jnp.arange(key_count, dtype=jnp.int32)
    allowed = (key_pos[None, :] <= query_pos[:, None]) & (key_pos[None, :] < length)
    weights_exp = jnp.where(allowed[None], jnp.exp(capped), jnp.float32(0.0))
    probs = (weights_exp / jnp.sum(weights_exp, axis=-1, keepdims=True)).astype(jnp.bfloat16)
    return jnp.einsum("hqk,kd->qhd", probs, value_rows, preferred_element_type=jnp.float32)


def on_device(
    inputs,
    lengths,
    gain_in,
    query_weight,
    key_weight,
    value_weight,
    output_weight,
    gain_post,
    gain_pre,
    gate_weight,
    up_weight,
):
    mp_index = lax.axis_index("mp")
    odd_flag = mp_index % 2 == 1
    query_width = query_weight.shape[1]
    own_width = key_weight.shape[1]
    ffn_width = gate_weight.shape[1]
    qkv_own = jnp.concatenate(
        [query_weight, key_weight, value_weight], axis=1
    ).astype(jnp.bfloat16)
    ffn_own = jnp.concatenate([gate_weight, up_weight], axis=1).astype(jnp.bfloat16)
    qkv_full = gather_dp(qkv_own)
    ffn_started = gather_dp_start(ffn_own)

    normed_local = rms_norm(inputs.astype(jnp.float32), gain_in).astype(jnp.bfloat16)
    normed = gather_mp(normed_local)
    group_tokens = normed.shape[0]
    slot = group_tokens

    raw = jnp.dot(normed, qkv_full, preferred_element_type=jnp.float32)
    raw_q = raw[:, :query_width]
    raw_kv_own = raw[:, query_width:]
    raw_kv_other = permute(raw_kv_own, "mp", lambda k: k ^ 1)
    raw_k = join_halves(raw_kv_own[:, :own_width], raw_kv_other[:, :own_width], odd_flag)
    raw_v = join_halves(raw_kv_own[:, own_width:], raw_kv_other[:, own_width:], odd_flag)

    head_size = raw_k.shape[1]
    local_heads = raw_q.shape[1] // head_size
    positions = jnp.arange(group_tokens, dtype=jnp.int32)
    length = lengths[0]
    live = positions < length
    queries = rotate_pairs(raw_q.reshape(group_tokens, local_heads, head_size), positions).astype(
        jnp.bfloat16
    )
    keys_rot = rotate_pairs(raw_k.reshape(group_tokens, 1, head_size), positions).reshape(
        group_tokens, head_size
    )
    keys_rot = jnp.where(live[:, None], keys_rot, jnp.float32(0.0)).astype(jnp.bfloat16)
    values_all = jnp.where(live[:, None], raw_v, jnp.float32(0.0)).astype(jnp.bfloat16)
    mixed = head_block(queries, keys_rot, values_all, slot, length)
    mixed = jnp.where(live[:, None, None], mixed, jnp.float32(0.0))
    attended = mixed.astype(jnp.bfloat16).reshape(slot, local_heads * head_size)
    partial = jnp.dot(attended, output_weight, preferred_element_type=jnp.float32).astype(
        jnp.bfloat16
    )
    ffn_started, partial = lax.optimization_barrier((ffn_started, partial))
    attn_rows = reduce_scatter_mp(partial)
    residual = (inputs.astype(jnp.float32) + rms_norm(attn_rows, gain_post)).astype(jnp.bfloat16)
    pre_local = rms_norm(residual.astype(jnp.float32), gain_pre).astype(jnp.bfloat16)
    ffn_full = gather_dp_finish(ffn_own, ffn_started)
    pre_ffn = gather_mp(pre_local)
    ffn_full, pre_ffn = lax.optimization_barrier((ffn_full, pre_ffn))
    both = jnp.dot(pre_ffn, ffn_full, preferred_element_type=jnp.float32)
    gate = both[:, :ffn_width]
    up_part = both[:, ffn_width:]
    hidden = (jax.nn.gelu(gate, approximate=True) * up_part).astype(jnp.bfloat16)
    offset = mp_index % 2 * own_width
    keys_out = lax.dynamic_slice_in_dim(keys_rot, offset, own_width, 1)
    values_out = lax.dynamic_slice_in_dim(values_all, offset, own_width, 1)
    return (residual, hidden, keys_out, values_out)


def solution(mesh):
    in_specs = (
        P(("dp", "mp"), None),
        P("dp"),
        P(),
        P("dp", "mp"),
        P("dp", "mp"),
        P("dp", "mp"),
        P("mp", None),
        P(),
        P(),
        P("dp", "mp"),
        P("dp", "mp"),
    )
    out_specs = (P(("dp", "mp"), None), P("dp", "mp"), P("dp", "mp"), P("dp", "mp"))
    return jax.shard_map(
        on_device, mesh=mesh, in_specs=in_specs, out_specs=out_specs, check_vma=False
    )
```

```python
import math

import jax
import jax.numpy as jnp
from jax import lax
from jax.sharding import PartitionSpec as P

query_scale = 1.0 / 12.0
soft_cap = 50.0


def permute(value, axis, target):
    return lax.ppermute(value, axis, [(k, target(k)) for k in range(lax.axis_size(axis))])


def gather_dp_start(value):
    count = lax.axis_size("dp")
    partner = permute(value, "dp", lambda k: k ^ 1)
    if count != 8:
        return (partner,)
    from_below = permute(value, "dp", lambda k: (k + 2) % count)
    from_above = permute(value, "dp", lambda k: (k - 2) % count)
    return (partner, from_below, from_above)


def gather_dp_finish(value, started, tie=None):
    count = lax.axis_size("dp")
    index = lax.axis_index("dp")
    if count != 8:
        full = gather_dp_direct(value, started[0])
        return full if tie is None else (full, tie)
    partner, from_below, from_above = started
    half = value.shape[0] // 2
    up = lambda k: (k + 2) % count
    down = lambda k: (k - 2) % count
    partner_below = permute(partner, "dp", up)
    partner_above = permute(partner, "dp", down)
    far_low = permute(from_below[:half], "dp", up)
    far_high = permute(from_above[half:], "dp", down)
    if tie is not None:
        (partner_below, partner_above, far_low, far_high), tie = lax.optimization_barrier(
            ((partner_below, partner_above, far_low, far_high), tie)
        )
    far_partner_low = permute(partner_below[:half], "dp", up)
    far_partner_high = permute(partner_above[half:], "dp", down)
    pieces = [
        (value, index),
        (partner, index ^ 1),
        (from_below, (index - 2) % count),
        (from_above, (index + 2) % count),
        (partner_below, ((index - 2) % count) ^ 1),
        (partner_above, ((index + 2) % count) ^ 1),
        (jnp.concatenate([far_low, far_high]), (index + 4) % count),
        (jnp.concatenate([far_partner_low, far_partner_high]), ((index + 4) % count) ^ 1),
    ]
    stacked = jnp.zeros((count,) + value.shape, value.dtype)
    for piece, where in pieces:
        stacked = lax.dynamic_update_index_in_dim(stacked, piece, where, 0)
    full = stacked.reshape(count * value.shape[0], value.shape[1])
    return full if tie is None else (full, tie)


def gather_dp(value):
    return gather_dp_finish(value, gather_dp_start(value))


def gather_dp_direct(value, partner):
    count = lax.axis_size("dp")
    index = lax.axis_index("dp")
    pieces = [(value, index), (partner, index ^ 1)]
    for step in range(1, count // 2):
        got = permute(value, "dp", lambda k, step=step: (k + 2 * step) % count)
        pieces.append((got, (index - 2 * step) % count))
    for step in range(1, count // 2):
        got = permute(partner, "dp", lambda k, step=step: (k + 2 * step) % count)
        pieces.append((got, ((index - 2 * step) % count) ^ 1))
    stacked = jnp.zeros((count,) + value.shape, value.dtype)
    for piece, where in pieces:
        stacked = lax.dynamic_update_index_in_dim(stacked, piece, where, 0)
    return stacked.reshape(count * value.shape[0], value.shape[1])


def pair_order(value, other, low_flag, axis):
    lower = jnp.where(low_flag, value, other)
    upper = jnp.where(low_flag, other, value)
    return jnp.stack([lower, upper], axis=axis)


def chip_orders(chip_bits):
    if chip_bits == 4:
        return [1, 3, 0, 2], [3, 1, 2, 0]
    return list(range(chip_bits)), list(range(chip_bits))


def bit_by_core(index, even_bits, odd_bits, step):
    return jnp.where(index % 2 == 0, even_bits[step], odd_bits[step])


def step_partner(even_bit, odd_bit):
    return lambda k: k ^ (2 << (even_bit if k % 2 == 0 else odd_bit))


def to_bit_order(stacked, axis_bits, chip_bits):
    return stacked.transpose([axis_bits.index(b) for b in range(chip_bits - 1, -1, -1)] + list(range(chip_bits, stacked.ndim)))


def gather_mp(value):
    count = lax.axis_size("mp")
    index = lax.axis_index("mp")
    other_core = index ^ 1
    chip_bits = (count // 2).bit_length() - 1
    even_bits, odd_bits = chip_orders(chip_bits)
    mine = value
    theirs = permute(value, "mp", lambda k: k ^ 1)
    for step in range(chip_bits):
        other = permute(mine, "mp", step_partner(even_bits[step], odd_bits[step]))
        passed = permute(other, "mp", lambda k: k ^ 1)
        bit = bit_by_core(index, even_bits, odd_bits, step)
        mine = pair_order(mine, other, (index >> (bit + 1)) % 2 == 0, 0)
        bit = bit_by_core(other_core, even_bits, odd_bits, step)
        theirs = pair_order(theirs, passed, (other_core >> (bit + 1)) % 2 == 0, 0)
    even_axes = list(reversed(even_bits))
    odd_axes = list(reversed(odd_bits))
    even = index % 2 == 0
    mine = jnp.where(
        even, to_bit_order(mine, even_axes, chip_bits), to_bit_order(mine, odd_axes, chip_bits)
    )
    theirs = jnp.where(
        even, to_bit_order(theirs, odd_axes, chip_bits), to_bit_order(theirs, even_axes, chip_bits)
    )
    stacked = pair_order(mine, theirs, even, chip_bits)
    return stacked.reshape(count * value.shape[0], value.shape[1])


def from_bit_order(blocks, step_bits, chip_bits):
    return blocks.transpose([chip_bits - 1 - b for b in step_bits] + list(range(chip_bits, blocks.ndim)))


def reduce_scatter_mp(value):
    count = lax.axis_size("mp")
    index = lax.axis_index("mp")
    chip_bits = (count // 2).bit_length() - 1
    rows = value.shape[0] // count
    even_bits, odd_bits = chip_orders(chip_bits)
    even_bits, odd_bits = even_bits[::-1], odd_bits[::-1]
    blocks = value.reshape([2] * chip_bits + [2, rows, value.shape[1]])
    core = index % 2
    mine = lax.dynamic_index_in_dim(blocks, core, chip_bits, keepdims=False)
    theirs = lax.dynamic_index_in_dim(blocks, 1 - core, chip_bits, keepdims=False)
    got = permute(theirs, "mp", lambda k: k ^ 1)
    total = mine.astype(jnp.float32) + got.astype(jnp.float32)
    total = jnp.where(
        index % 2 == 0,
        from_bit_order(total, even_bits, chip_bits),
        from_bit_order(total, odd_bits, chip_bits),
    )
    for step in range(chip_bits):
        bit = bit_by_core(index, even_bits, odd_bits, step)
        mine_bit = (index >> (bit + 1)) % 2
        keep = lax.dynamic_index_in_dim(total, mine_bit, 0, keepdims=False)
        send = lax.dynamic_index_in_dim(total, 1 - mine_bit, 0, keepdims=False)
        got = permute(
            send.astype(jnp.bfloat16), "mp", step_partner(even_bits[step], odd_bits[step])
        )
        total = keep + got.astype(jnp.float32)
    return total


def rms_norm(values, gain):
    mean_sq = jnp.mean(values * values, axis=-1, keepdims=True)
    return values * lax.rsqrt(mean_sq + 1e-06) * gain


def rotate_pairs(values, positions):
    half_size = values.shape[-1] // 2
    freqs = jnp.exp(
        jnp.arange(half_size, dtype=jnp.float32) * (-2.0 * math.log(10000.0) / values.shape[-1])
    )
    angles = positions.astype(jnp.float32)[:, None] * freqs[None, :]
    cosine = jnp.cos(angles)[:, None, :]
    sine = jnp.sin(angles)[:, None, :]
    first = values[..., :half_size]
    second = values[..., half_size:]
    return jnp.concatenate(
        [first * cosine - second * sine, second * cosine + first * sine], axis=-1
    )


def join_halves(own_half, other_half, odd_flag):
    lower_first = jnp.concatenate([own_half, other_half], axis=1)
    upper_first = jnp.concatenate([other_half, own_half], axis=1)
    return jnp.where(odd_flag, upper_first, lower_first)


def head_block(query_rows, key_rows, value_rows, key_count, length):
    scores = (
        jnp.einsum("qhd,kd->hqk", query_rows, key_rows, preferred_element_type=jnp.float32)
        * query_scale
    )
    capped = soft_cap * jnp.tanh(scores / soft_cap)
    query_pos = jnp.arange(query_rows.shape[0], dtype=jnp.int32)
    key_pos = jnp.arange(key_count, dtype=jnp.int32)
    allowed = (key_pos[None, :] <= query_pos[:, None]) & (key_pos[None, :] < length)
    weights_exp = jnp.where(allowed[None], jnp.exp(capped), jnp.float32(0.0))
    probs = (weights_exp / jnp.sum(weights_exp, axis=-1, keepdims=True)).astype(jnp.bfloat16)
    return jnp.einsum("hqk,kd->qhd", probs, value_rows, preferred_element_type=jnp.float32)


def on_device(
    inputs,
    lengths,
    gain_in,
    query_weight,
    key_weight,
    value_weight,
    output_weight,
    gain_post,
    gain_pre,
    gate_weight,
    up_weight,
):
    mp_index = lax.axis_index("mp")
    odd_flag = mp_index % 2 == 1
    query_width = query_weight.shape[1]
    own_width = key_weight.shape[1]
    ffn_width = gate_weight.shape[1]
    qkv_own = jnp.concatenate(
        [query_weight, key_weight, value_weight], axis=1
    ).astype(jnp.bfloat16)
    ffn_own = jnp.concatenate([gate_weight, up_weight], axis=1).astype(jnp.bfloat16)
    qkv_full = gather_dp(qkv_own)
    ffn_started = gather_dp_start(ffn_own)

    normed_local = rms_norm(inputs.astype(jnp.float32), gain_in).astype(jnp.bfloat16)
    normed = gather_mp(normed_local)
    group_tokens = normed.shape[0]
    slot = group_tokens

    raw = jnp.dot(normed, qkv_full, preferred_element_type=jnp.float32)
    raw_q = raw[:, :query_width]
    raw_kv_own = raw[:, query_width:]
    raw_kv_other = permute(raw_kv_own, "mp", lambda k: k ^ 1)
    raw_k = join_halves(raw_kv_own[:, :own_width], raw_kv_other[:, :own_width], odd_flag)
    raw_v = join_halves(raw_kv_own[:, own_width:], raw_kv_other[:, own_width:], odd_flag)

    head_size = raw_k.shape[1]
    local_heads = raw_q.shape[1] // head_size
    positions = jnp.arange(group_tokens, dtype=jnp.int32)
    length = lengths[0]
    live = positions < length
    queries = rotate_pairs(raw_q.reshape(group_tokens, local_heads, head_size), positions).astype(
        jnp.bfloat16
    )
    keys_rot = rotate_pairs(raw_k.reshape(group_tokens, 1, head_size), positions).reshape(
        group_tokens, head_size
    )
    keys_rot = jnp.where(live[:, None], keys_rot, jnp.float32(0.0)).astype(jnp.bfloat16)
    values_all = jnp.where(live[:, None], raw_v, jnp.float32(0.0)).astype(jnp.bfloat16)
    mixed = head_block(queries, keys_rot, values_all, slot, length)
    mixed = jnp.where(live[:, None, None], mixed, jnp.float32(0.0))
    attended = mixed.astype(jnp.bfloat16).reshape(slot, local_heads * head_size)
    partial = jnp.dot(attended, output_weight, preferred_element_type=jnp.float32).astype(
        jnp.bfloat16
    )
    ffn_started, partial = lax.optimization_barrier((ffn_started, partial))
    attn_rows = reduce_scatter_mp(partial)
    residual = (inputs.astype(jnp.float32) + rms_norm(attn_rows, gain_post)).astype(jnp.bfloat16)
    pre_local = rms_norm(residual.astype(jnp.float32), gain_pre).astype(jnp.bfloat16)
    ffn_full = gather_dp_finish(ffn_own, ffn_started)
    pre_ffn = gather_mp(pre_local)
    ffn_full, pre_ffn = lax.optimization_barrier((ffn_full, pre_ffn))
    both = jnp.dot(pre_ffn, ffn_full, preferred_element_type=jnp.float32)
    gate = both[:, :ffn_width]
    up_part = both[:, ffn_width:]
    hidden = (jax.nn.gelu(gate, approximate=True) * up_part).astype(jnp.bfloat16)
    offset = mp_index % 2 * own_width
    keys_out = lax.dynamic_slice_in_dim(keys_rot, offset, own_width, 1)
    values_out = lax.dynamic_slice_in_dim(values_all, offset, own_width, 1)
    return (residual, hidden, keys_out, values_out)


def solution(mesh):
    in_specs = (
        P(("dp", "mp"), None),
        P("dp"),
        P(),
        P("dp", "mp"),
        P("dp", "mp"),
        P("dp", "mp"),
        P("mp", None),
        P(),
        P(),
        P("dp", "mp"),
        P("dp", "mp"),
    )
    out_specs = (P(("dp", "mp"), None), P("dp", "mp"), P("dp", "mp"), P("dp", "mp"))
    return jax.shard_map(
        on_device, mesh=mesh, in_specs=in_specs, out_specs=out_specs, check_vma=False
    )
```

```python
import math

import jax
import jax.numpy as jnp
from jax import lax
from jax.sharding import PartitionSpec as P

query_scale = 1.0 / 12.0
soft_cap = 50.0


def permute(value, axis, target):
    return lax.ppermute(value, axis, [(k, target(k)) for k in range(lax.axis_size(axis))])


def gather_dp_start(value):
    count = lax.axis_size("dp")
    partner = permute(value, "dp", lambda k: k ^ 1)
    if count != 8:
        return (partner,)
    from_below = permute(value, "dp", lambda k: (k + 2) % count)
    from_above = permute(value, "dp", lambda k: (k - 2) % count)
    return (partner, from_below, from_above)


def gather_dp_finish(value, started, tie=None):
    count = lax.axis_size("dp")
    index = lax.axis_index("dp")
    if count != 8:
        full = gather_dp_direct(value, started[0])
        return full if tie is None else (full, tie)
    partner, from_below, from_above = started
    half = value.shape[0] // 2
    up = lambda k: (k + 2) % count
    down = lambda k: (k - 2) % count
    partner_below = permute(partner, "dp", up)
    partner_above = permute(partner, "dp", down)
    far_low = permute(from_below[:half], "dp", up)
    far_high = permute(from_above[half:], "dp", down)
    if tie is not None:
        (partner_below, partner_above, far_low, far_high), tie = lax.optimization_barrier(
            ((partner_below, partner_above, far_low, far_high), tie)
        )
    far_partner_low = permute(partner_below[:half], "dp", up)
    far_partner_high = permute(partner_above[half:], "dp", down)
    pieces = [
        (value, index),
        (partner, index ^ 1),
        (from_below, (index - 2) % count),
        (from_above, (index + 2) % count),
        (partner_below, ((index - 2) % count) ^ 1),
        (partner_above, ((index + 2) % count) ^ 1),
        (jnp.concatenate([far_low, far_high]), (index + 4) % count),
        (jnp.concatenate([far_partner_low, far_partner_high]), ((index + 4) % count) ^ 1),
    ]
    stacked = jnp.zeros((count,) + value.shape, value.dtype)
    for piece, where in pieces:
        stacked = lax.dynamic_update_index_in_dim(stacked, piece, where, 0)
    full = stacked.reshape(count * value.shape[0], value.shape[1])
    return full if tie is None else (full, tie)


def gather_dp(value):
    return gather_dp_finish(value, gather_dp_start(value))


def gather_dp_direct(value, partner):
    count = lax.axis_size("dp")
    index = lax.axis_index("dp")
    pieces = [(value, index), (partner, index ^ 1)]
    for step in range(1, count // 2):
        got = permute(value, "dp", lambda k, step=step: (k + 2 * step) % count)
        pieces.append((got, (index - 2 * step) % count))
    for step in range(1, count // 2):
        got = permute(partner, "dp", lambda k, step=step: (k + 2 * step) % count)
        pieces.append((got, ((index - 2 * step) % count) ^ 1))
    stacked = jnp.zeros((count,) + value.shape, value.dtype)
    for piece, where in pieces:
        stacked = lax.dynamic_update_index_in_dim(stacked, piece, where, 0)
    return stacked.reshape(count * value.shape[0], value.shape[1])


def pair_order(value, other, low_flag, axis):
    lower = jnp.where(low_flag, value, other)
    upper = jnp.where(low_flag, other, value)
    return jnp.stack([lower, upper], axis=axis)


def chip_orders(chip_bits):
    if chip_bits == 4:
        return [1, 3, 0, 2], [3, 1, 2, 0]
    return list(range(chip_bits)), list(range(chip_bits))


def bit_by_core(index, even_bits, odd_bits, step):
    return jnp.where(index % 2 == 0, even_bits[step], odd_bits[step])


def step_partner(even_bit, odd_bit):
    return lambda k: k ^ (2 << (even_bit if k % 2 == 0 else odd_bit))


def to_bit_order(stacked, axis_bits, chip_bits):
    return stacked.transpose([axis_bits.index(b) for b in range(chip_bits - 1, -1, -1)] + list(range(chip_bits, stacked.ndim)))


def gather_mp(value):
    count = lax.axis_size("mp")
    index = lax.axis_index("mp")
    other_core = index ^ 1
    chip_bits = (count // 2).bit_length() - 1
    even_bits, odd_bits = chip_orders(chip_bits)
    mine = value
    theirs = permute(value, "mp", lambda k: k ^ 1)
    for step in range(chip_bits):
        other = permute(mine, "mp", step_partner(even_bits[step], odd_bits[step]))
        passed = permute(other, "mp", lambda k: k ^ 1)
        bit = bit_by_core(index, even_bits, odd_bits, step)
        mine = pair_order(mine, other, (index >> (bit + 1)) % 2 == 0, 0)
        bit = bit_by_core(other_core, even_bits, odd_bits, step)
        theirs = pair_order(theirs, passed, (other_core >> (bit + 1)) % 2 == 0, 0)
    even_axes = list(reversed(even_bits))
    odd_axes = list(reversed(odd_bits))
    even = index % 2 == 0
    mine = jnp.where(
        even, to_bit_order(mine, even_axes, chip_bits), to_bit_order(mine, odd_axes, chip_bits)
    )
    theirs = jnp.where(
        even, to_bit_order(theirs, odd_axes, chip_bits), to_bit_order(theirs, even_axes, chip_bits)
    )
    stacked = pair_order(mine, theirs, even, chip_bits)
    return stacked.reshape(count * value.shape[0], value.shape[1])


def from_bit_order(blocks, step_bits, chip_bits):
    return blocks.transpose([chip_bits - 1 - b for b in step_bits] + list(range(chip_bits, blocks.ndim)))


def reduce_scatter_mp(value):
    count = lax.axis_size("mp")
    index = lax.axis_index("mp")
    other_core = index ^ 1
    chip_bits = (count // 2).bit_length() - 1
    rows = value.shape[0] // count
    even_bits, odd_bits = chip_orders(chip_bits)
    even_bits, odd_bits = even_bits[::-1], odd_bits[::-1]
    blocks = value.reshape([2] * chip_bits + [2, rows, value.shape[1]])
    core = index % 2
    even = core == 0
    mine = lax.dynamic_index_in_dim(blocks, core, chip_bits, keepdims=False)
    theirs = lax.dynamic_index_in_dim(blocks, 1 - core, chip_bits, keepdims=False)
    mine = jnp.where(
        even, from_bit_order(mine, even_bits, chip_bits), from_bit_order(mine, odd_bits, chip_bits)
    )
    theirs = jnp.where(
        even, from_bit_order(theirs, odd_bits, chip_bits), from_bit_order(theirs, even_bits, chip_bits)
    )
    shares = []
    for step in range(chip_bits):
        bit = bit_by_core(other_core, even_bits, odd_bits, step)
        kept = (other_core >> (bit + 1)) % 2
        shares.append(lax.dynamic_index_in_dim(theirs, 1 - kept, 0, keepdims=False))
        theirs = lax.dynamic_index_in_dim(theirs, kept, 0, keepdims=False)
    shares.append(theirs)
    total = mine.astype(jnp.float32)
    for step in range(chip_bits):
        share = permute(shares[step], "mp", lambda k: k ^ 1)
        bit = bit_by_core(index, even_bits, odd_bits, step)
        mine_bit = (index >> (bit + 1)) % 2
        keep = lax.dynamic_index_in_dim(total, mine_bit, 0, keepdims=False)
        send = lax.dynamic_index_in_dim(total, 1 - mine_bit, 0, keepdims=False)
        send = send + share.astype(jnp.float32)
        got = permute(
            send.astype(jnp.bfloat16), "mp", step_partner(even_bits[step], odd_bits[step])
        )
        total = keep + got.astype(jnp.float32)
    share = permute(shares[chip_bits], "mp", lambda k: k ^ 1)
    return total + share.astype(jnp.float32)


def rms_norm(values, gain):
    mean_sq = jnp.mean(values * values, axis=-1, keepdims=True)
    return values * lax.rsqrt(mean_sq + 1e-06) * gain


def rotate_pairs(values, positions):
    half_size = values.shape[-1] // 2
    freqs = jnp.exp(
        jnp.arange(half_size, dtype=jnp.float32) * (-2.0 * math.log(10000.0) / values.shape[-1])
    )
    angles = positions.astype(jnp.float32)[:, None] * freqs[None, :]
    cosine = jnp.cos(angles)[:, None, :]
    sine = jnp.sin(angles)[:, None, :]
    first = values[..., :half_size]
    second = values[..., half_size:]
    return jnp.concatenate(
        [first * cosine - second * sine, second * cosine + first * sine], axis=-1
    )


def join_halves(own_half, other_half, odd_flag):
    lower_first = jnp.concatenate([own_half, other_half], axis=1)
    upper_first = jnp.concatenate([other_half, own_half], axis=1)
    return jnp.where(odd_flag, upper_first, lower_first)


def head_block(query_rows, key_rows, value_rows, key_count, length):
    scores = (
        jnp.einsum("qhd,kd->hqk", query_rows, key_rows, preferred_element_type=jnp.float32)
        * query_scale
    )
    capped = soft_cap * jnp.tanh(scores / soft_cap)
    query_pos = jnp.arange(query_rows.shape[0], dtype=jnp.int32)
    key_pos = jnp.arange(key_count, dtype=jnp.int32)
    allowed = (key_pos[None, :] <= query_pos[:, None]) & (key_pos[None, :] < length)
    weights_exp = jnp.where(allowed[None], jnp.exp(capped), jnp.float32(0.0))
    probs = (weights_exp / jnp.sum(weights_exp, axis=-1, keepdims=True)).astype(jnp.bfloat16)
    return jnp.einsum("hqk,kd->qhd", probs, value_rows, preferred_element_type=jnp.float32)


def on_device(
    inputs,
    lengths,
    gain_in,
    query_weight,
    key_weight,
    value_weight,
    output_weight,
    gain_post,
    gain_pre,
    gate_weight,
    up_weight,
):
    mp_index = lax.axis_index("mp")
    odd_flag = mp_index % 2 == 1
    query_width = query_weight.shape[1]
    own_width = key_weight.shape[1]
    ffn_width = gate_weight.shape[1]
    qkv_own = jnp.concatenate(
        [query_weight, key_weight, value_weight], axis=1
    ).astype(jnp.bfloat16)
    ffn_own = jnp.concatenate([gate_weight, up_weight], axis=1).astype(jnp.bfloat16)
    qkv_full = gather_dp(qkv_own)
    ffn_started = gather_dp_start(ffn_own)

    normed_local = rms_norm(inputs.astype(jnp.float32), gain_in).astype(jnp.bfloat16)
    normed = gather_mp(normed_local)
    group_tokens = normed.shape[0]
    slot = group_tokens

    raw = jnp.dot(normed, qkv_full, preferred_element_type=jnp.float32)
    raw_q = raw[:, :query_width]
    raw_kv_own = raw[:, query_width:]
    raw_kv_other = permute(raw_kv_own, "mp", lambda k: k ^ 1)
    raw_k = join_halves(raw_kv_own[:, :own_width], raw_kv_other[:, :own_width], odd_flag)
    raw_v = join_halves(raw_kv_own[:, own_width:], raw_kv_other[:, own_width:], odd_flag)

    head_size = raw_k.shape[1]
    local_heads = raw_q.shape[1] // head_size
    positions = jnp.arange(group_tokens, dtype=jnp.int32)
    length = lengths[0]
    live = positions < length
    queries = rotate_pairs(raw_q.reshape(group_tokens, local_heads, head_size), positions).astype(
        jnp.bfloat16
    )
    keys_rot = rotate_pairs(raw_k.reshape(group_tokens, 1, head_size), positions).reshape(
        group_tokens, head_size
    )
    keys_rot = jnp.where(live[:, None], keys_rot, jnp.float32(0.0)).astype(jnp.bfloat16)
    values_all = jnp.where(live[:, None], raw_v, jnp.float32(0.0)).astype(jnp.bfloat16)
    mixed = head_block(queries, keys_rot, values_all, slot, length)
    mixed = jnp.where(live[:, None, None], mixed, jnp.float32(0.0))
    attended = mixed.astype(jnp.bfloat16).reshape(slot, local_heads * head_size)
    partial = jnp.dot(attended, output_weight, preferred_element_type=jnp.float32).astype(
        jnp.bfloat16
    )
    ffn_started, partial = lax.optimization_barrier((ffn_started, partial))
    attn_rows = reduce_scatter_mp(partial)
    residual = (inputs.astype(jnp.float32) + rms_norm(attn_rows, gain_post)).astype(jnp.bfloat16)
    pre_local = rms_norm(residual.astype(jnp.float32), gain_pre).astype(jnp.bfloat16)
    ffn_full = gather_dp_finish(ffn_own, ffn_started)
    pre_ffn = gather_mp(pre_local)
    ffn_full, pre_ffn = lax.optimization_barrier((ffn_full, pre_ffn))
    both = jnp.dot(pre_ffn, ffn_full, preferred_element_type=jnp.float32)
    gate = both[:, :ffn_width]
    up_part = both[:, ffn_width:]
    hidden = (jax.nn.gelu(gate, approximate=True) * up_part).astype(jnp.bfloat16)
    offset = mp_index % 2 * own_width
    keys_out = lax.dynamic_slice_in_dim(keys_rot, offset, own_width, 1)
    values_out = lax.dynamic_slice_in_dim(values_all, offset, own_width, 1)
    return (residual, hidden, keys_out, values_out)


def solution(mesh):
    in_specs = (
        P(("dp", "mp"), None),
        P("dp"),
        P(),
        P("dp", "mp"),
        P("dp", "mp"),
        P("dp", "mp"),
        P("mp", None),
        P(),
        P(),
        P("dp", "mp"),
        P("dp", "mp"),
    )
    out_specs = (P(("dp", "mp"), None), P("dp", "mp"), P("dp", "mp"), P("dp", "mp"))
    return jax.shard_map(
        on_device, mesh=mesh, in_specs=in_specs, out_specs=out_specs, check_vma=False
    )
```

```python
import math

import jax
import jax.numpy as jnp
from jax import lax
from jax.sharding import PartitionSpec as P

query_scale = 1.0 / 12.0
soft_cap = 50.0


def permute(value, axis, target):
    return lax.ppermute(value, axis, [(k, target(k)) for k in range(lax.axis_size(axis))])


def gather_dp_start(value):
    count = lax.axis_size("dp")
    partner = permute(value, "dp", lambda k: k ^ 1)
    if count != 8:
        return (partner,)
    from_below = permute(value, "dp", lambda k: (k + 2) % count)
    from_above = permute(value, "dp", lambda k: (k - 2) % count)
    return (partner, from_below, from_above)


def gather_dp_finish(value, started, tie=None):
    count = lax.axis_size("dp")
    index = lax.axis_index("dp")
    if count != 8:
        full = gather_dp_direct(value, started[0])
        return full if tie is None else (full, tie)
    partner, from_below, from_above = started
    half = value.shape[0] // 2
    up = lambda k: (k + 2) % count
    down = lambda k: (k - 2) % count
    partner_below = permute(partner, "dp", up)
    partner_above = permute(partner, "dp", down)
    far_low = permute(from_below[:half], "dp", up)
    far_high = permute(from_above[half:], "dp", down)
    if tie is not None:
        (partner_below, partner_above, far_low, far_high), tie = lax.optimization_barrier(
            ((partner_below, partner_above, far_low, far_high), tie)
        )
    far_partner_low = permute(partner_below[:half], "dp", up)
    far_partner_high = permute(partner_above[half:], "dp", down)
    pieces = [
        (value, index),
        (partner, index ^ 1),
        (from_below, (index - 2) % count),
        (from_above, (index + 2) % count),
        (partner_below, ((index - 2) % count) ^ 1),
        (partner_above, ((index + 2) % count) ^ 1),
        (jnp.concatenate([far_low, far_high]), (index + 4) % count),
        (jnp.concatenate([far_partner_low, far_partner_high]), ((index + 4) % count) ^ 1),
    ]
    stacked = jnp.zeros((count,) + value.shape, value.dtype)
    for piece, where in pieces:
        stacked = lax.dynamic_update_index_in_dim(stacked, piece, where, 0)
    full = stacked.reshape(count * value.shape[0], value.shape[1])
    return full if tie is None else (full, tie)


def gather_dp(value):
    return gather_dp_finish(value, gather_dp_start(value))


def gather_dp_direct(value, partner):
    count = lax.axis_size("dp")
    index = lax.axis_index("dp")
    pieces = [(value, index), (partner, index ^ 1)]
    for step in range(1, count // 2):
        got = permute(value, "dp", lambda k, step=step: (k + 2 * step) % count)
        pieces.append((got, (index - 2 * step) % count))
    for step in range(1, count // 2):
        got = permute(partner, "dp", lambda k, step=step: (k + 2 * step) % count)
        pieces.append((got, ((index - 2 * step) % count) ^ 1))
    stacked = jnp.zeros((count,) + value.shape, value.dtype)
    for piece, where in pieces:
        stacked = lax.dynamic_update_index_in_dim(stacked, piece, where, 0)
    return stacked.reshape(count * value.shape[0], value.shape[1])


def pair_order(value, other, low_flag, axis):
    lower = jnp.where(low_flag, value, other)
    upper = jnp.where(low_flag, other, value)
    return jnp.stack([lower, upper], axis=axis)


def chip_orders(chip_bits):
    if chip_bits == 4:
        return [1, 3, 0, 2], [3, 1, 2, 0]
    return list(range(chip_bits)), list(range(chip_bits))


def bit_by_core(index, even_bits, odd_bits, step):
    return jnp.where(index % 2 == 0, even_bits[step], odd_bits[step])


def step_partner(even_bit, odd_bit):
    return lambda k: k ^ (2 << (even_bit if k % 2 == 0 else odd_bit))


def to_bit_order(stacked, axis_bits, chip_bits):
    return stacked.transpose([axis_bits.index(b) for b in range(chip_bits - 1, -1, -1)] + list(range(chip_bits, stacked.ndim)))


def gather_mp(value):
    count = lax.axis_size("mp")
    index = lax.axis_index("mp")
    other_core = index ^ 1
    chip_bits = (count // 2).bit_length() - 1
    even_bits, odd_bits = chip_orders(chip_bits)
    mine = value
    theirs = permute(value, "mp", lambda k: k ^ 1)
    for step in range(chip_bits):
        other = permute(mine, "mp", step_partner(even_bits[step], odd_bits[step]))
        passed = permute(other, "mp", lambda k: k ^ 1)
        bit = bit_by_core(index, even_bits, odd_bits, step)
        mine = pair_order(mine, other, (index >> (bit + 1)) % 2 == 0, 0)
        bit = bit_by_core(other_core, even_bits, odd_bits, step)
        theirs = pair_order(theirs, passed, (other_core >> (bit + 1)) % 2 == 0, 0)
    even_axes = list(reversed(even_bits))
    odd_axes = list(reversed(odd_bits))
    even = index % 2 == 0
    mine = jnp.where(
        even, to_bit_order(mine, even_axes, chip_bits), to_bit_order(mine, odd_axes, chip_bits)
    )
    theirs = jnp.where(
        even, to_bit_order(theirs, odd_axes, chip_bits), to_bit_order(theirs, even_axes, chip_bits)
    )
    stacked = pair_order(mine, theirs, even, chip_bits)
    return stacked.reshape(count * value.shape[0], value.shape[1])


def from_bit_order(blocks, step_bits, chip_bits):
    return blocks.transpose([chip_bits - 1 - b for b in step_bits] + list(range(chip_bits, blocks.ndim)))


def reduce_scatter_mp(value):
    count = lax.axis_size("mp")
    index = lax.axis_index("mp")
    other_core = index ^ 1
    chip_bits = (count // 2).bit_length() - 1
    rows = value.shape[0] // count
    even_bits, odd_bits = chip_orders(chip_bits)
    even_bits, odd_bits = even_bits[::-1], odd_bits[::-1]
    blocks = value.reshape([2] * chip_bits + [2, rows, value.shape[1]])
    core = index % 2
    even = core == 0
    mine = lax.dynamic_index_in_dim(blocks, core, chip_bits, keepdims=False)
    theirs = lax.dynamic_index_in_dim(blocks, 1 - core, chip_bits, keepdims=False)
    mine = jnp.where(
        even, from_bit_order(mine, even_bits, chip_bits), from_bit_order(mine, odd_bits, chip_bits)
    )
    theirs = jnp.where(
        even, from_bit_order(theirs, odd_bits, chip_bits), from_bit_order(theirs, even_bits, chip_bits)
    )
    shares = []
    for step in range(chip_bits):
        bit = bit_by_core(other_core, even_bits, odd_bits, step)
        kept = (other_core >> (bit + 1)) % 2
        shares.append(lax.dynamic_index_in_dim(theirs, 1 - kept, 0, keepdims=False))
        theirs = lax.dynamic_index_in_dim(theirs, kept, 0, keepdims=False)
    shares.append(theirs)
    total = mine.astype(jnp.float32)
    for step in range(chip_bits):
        share = permute(shares[step], "mp", lambda k: k ^ 1)
        bit = bit_by_core(index, even_bits, odd_bits, step)
        mine_bit = (index >> (bit + 1)) % 2
        keep = lax.dynamic_index_in_dim(total, mine_bit, 0, keepdims=False)
        send = lax.dynamic_index_in_dim(total, 1 - mine_bit, 0, keepdims=False)
        send = send + share.astype(jnp.float32)
        got = permute(
            send.astype(jnp.bfloat16), "mp", step_partner(even_bits[step], odd_bits[step])
        )
        total = keep + got.astype(jnp.float32)
    share = permute(shares[chip_bits], "mp", lambda k: k ^ 1)
    return total + share.astype(jnp.float32)


def rms_norm(values, gain):
    mean_sq = jnp.mean(values * values, axis=-1, keepdims=True)
    return values * lax.rsqrt(mean_sq + 1e-06) * gain


def rotate_pairs(values, positions):
    half_size = values.shape[-1] // 2
    freqs = jnp.exp(
        jnp.arange(half_size, dtype=jnp.float32) * (-2.0 * math.log(10000.0) / values.shape[-1])
    )
    angles = positions.astype(jnp.float32)[:, None] * freqs[None, :]
    cosine = jnp.cos(angles)[:, None, :]
    sine = jnp.sin(angles)[:, None, :]
    first = values[..., :half_size]
    second = values[..., half_size:]
    return jnp.concatenate(
        [first * cosine - second * sine, second * cosine + first * sine], axis=-1
    )


def join_halves(own_half, other_half, odd_flag):
    lower_first = jnp.concatenate([own_half, other_half], axis=1)
    upper_first = jnp.concatenate([other_half, own_half], axis=1)
    return jnp.where(odd_flag, upper_first, lower_first)


def head_block(query_rows, key_rows, value_rows, key_count, length):
    scores = (
        jnp.einsum("qhd,kd->hqk", query_rows, key_rows, preferred_element_type=jnp.float32)
        * query_scale
    )
    capped = soft_cap * jnp.tanh(scores / soft_cap)
    query_pos = jnp.arange(query_rows.shape[0], dtype=jnp.int32)
    key_pos = jnp.arange(key_count, dtype=jnp.int32)
    allowed = (key_pos[None, :] <= query_pos[:, None]) & (key_pos[None, :] < length)
    weights_exp = jnp.where(allowed[None], jnp.exp(capped), jnp.float32(0.0))
    probs = (weights_exp / jnp.sum(weights_exp, axis=-1, keepdims=True)).astype(jnp.bfloat16)
    return jnp.einsum("hqk,kd->qhd", probs, value_rows, preferred_element_type=jnp.float32)


def on_device(
    inputs,
    lengths,
    gain_in,
    query_weight,
    key_weight,
    value_weight,
    output_weight,
    gain_post,
    gain_pre,
    gate_weight,
    up_weight,
):
    mp_index = lax.axis_index("mp")
    odd_flag = mp_index % 2 == 1
    query_width = query_weight.shape[1]
    own_width = key_weight.shape[1]
    ffn_width = gate_weight.shape[1]
    qkv_own = jnp.concatenate(
        [query_weight, key_weight, value_weight], axis=1
    ).astype(jnp.bfloat16)
    ffn_own = jnp.concatenate([gate_weight, up_weight], axis=1).astype(jnp.bfloat16)
    qkv_full = gather_dp(qkv_own)

    normed_local = rms_norm(inputs.astype(jnp.float32), gain_in).astype(jnp.bfloat16)
    normed = gather_mp(normed_local)
    ffn_own, normed = lax.optimization_barrier((ffn_own, normed))
    ffn_started = gather_dp_start(ffn_own)
    group_tokens = normed.shape[0]
    slot = group_tokens

    raw = jnp.dot(normed, qkv_full, preferred_element_type=jnp.float32)
    raw_q = raw[:, :query_width]
    raw_kv_own = raw[:, query_width:]
    raw_kv_other = permute(raw_kv_own, "mp", lambda k: k ^ 1)
    raw_k = join_halves(raw_kv_own[:, :own_width], raw_kv_other[:, :own_width], odd_flag)
    raw_v = join_halves(raw_kv_own[:, own_width:], raw_kv_other[:, own_width:], odd_flag)

    head_size = raw_k.shape[1]
    local_heads = raw_q.shape[1] // head_size
    positions = jnp.arange(group_tokens, dtype=jnp.int32)
    length = lengths[0]
    live = positions < length
    queries = rotate_pairs(raw_q.reshape(group_tokens, local_heads, head_size), positions).astype(
        jnp.bfloat16
    )
    keys_rot = rotate_pairs(raw_k.reshape(group_tokens, 1, head_size), positions).reshape(
        group_tokens, head_size
    )
    keys_rot = jnp.where(live[:, None], keys_rot, jnp.float32(0.0)).astype(jnp.bfloat16)
    values_all = jnp.where(live[:, None], raw_v, jnp.float32(0.0)).astype(jnp.bfloat16)
    mixed = head_block(queries, keys_rot, values_all, slot, length)
    mixed = jnp.where(live[:, None, None], mixed, jnp.float32(0.0))
    attended = mixed.astype(jnp.bfloat16).reshape(slot, local_heads * head_size)
    partial = jnp.dot(attended, output_weight, preferred_element_type=jnp.float32).astype(
        jnp.bfloat16
    )
    ffn_started, partial = lax.optimization_barrier((ffn_started, partial))
    attn_rows = reduce_scatter_mp(partial)
    residual = (inputs.astype(jnp.float32) + rms_norm(attn_rows, gain_post)).astype(jnp.bfloat16)
    pre_local = rms_norm(residual.astype(jnp.float32), gain_pre).astype(jnp.bfloat16)
    ffn_full = gather_dp_finish(ffn_own, ffn_started)
    pre_ffn = gather_mp(pre_local)
    ffn_full, pre_ffn = lax.optimization_barrier((ffn_full, pre_ffn))
    both = jnp.dot(pre_ffn, ffn_full, preferred_element_type=jnp.float32)
    gate = both[:, :ffn_width]
    up_part = both[:, ffn_width:]
    hidden = (jax.nn.gelu(gate, approximate=True) * up_part).astype(jnp.bfloat16)
    offset = mp_index % 2 * own_width
    keys_out = lax.dynamic_slice_in_dim(keys_rot, offset, own_width, 1)
    values_out = lax.dynamic_slice_in_dim(values_all, offset, own_width, 1)
    return (residual, hidden, keys_out, values_out)


def solution(mesh):
    in_specs = (
        P(("dp", "mp"), None),
        P("dp"),
        P(),
        P("dp", "mp"),
        P("dp", "mp"),
        P("dp", "mp"),
        P("mp", None),
        P(),
        P(),
        P("dp", "mp"),
        P("dp", "mp"),
    )
    out_specs = (P(("dp", "mp"), None), P("dp", "mp"), P("dp", "mp"), P("dp", "mp"))
    return jax.shard_map(
        on_device, mesh=mesh, in_specs=in_specs, out_specs=out_specs, check_vma=False
    )
```
